128 devices in a mesh: ctx: 16 (over z, y), head: 8 (over x, core).
Axes of the slice: x: 4, y: 4, z: 4, core: 2. Of those that a mesh axis runs over, the one named last changes fastest.
Arguments:
- lin_query: bfloat16 [3, 8192, 8192], P(None, 'ctx', 'head'), may hold values from -6 to 6
- lin_key: bfloat16 [3, 8192, 8192], P(None, 'ctx', 'head'), may hold values from -6 to 6
- lin_value: bfloat16 [3, 8192, 8192], P(None, 'ctx', 'head'), may hold values from -21 to 21
- lin_gain: float32 [8192], P('head'), may hold values from 0.5 to 1.5
- sparse_query: bfloat16 [3, 8192, 8192], P(None, 'ctx', 'head'), may hold values from -52 to 52
- sparse_key: bfloat16 [3, 8192, 1024], P(None, 'ctx', 'head'), may hold values from -4 to 4
- sparse_value: bfloat16 [3, 8192, 1024], P(None, 'ctx', 'head'), may hold values from -6 to 6
- block_lists: int32 [3, 128, 8], P(None, 'ctx'), may hold values from 0 to 127, as said below
Outputs:
- lin_out: bfloat16 [3, 8192, 8192], P(None, 'ctx', 'head')
- sparse_out: bfloat16 [3, 8192, 8192], P(None, 'ctx', 'head')
The draws below stay inside these ranges and needn't reach their ends.
Inputs may be any that keep to these rules, and one draw needn't show every extreme that they name: `block_lists`: row b of a sequence lists b itself first, then 8 - 1 other distinct blocks, each either on the same ctx index as b or on a lower one. Over the 8 query blocks of one ctx index, the distinct blocks listed from any one other ctx index number at most 2; every draw has such a pair with exactly 2.
All inputs are finite; a program needn't handle non-finite values.
Results may differ from the reference program's by a relative error of at most 0.0049.
Values may be sent and summed in bfloat16 or wider, within the bound.
No kernel may reach another device: no remote copies, remote signals or barrier semaphores. Data moves between devices by JAX's collectives and lax.ppermute only.
A program may use at most 192 MiB of HBM per device.

```python
import math
import jax
import jax.numpy as jnp
from jax import lax

HEADS = 64
HEAD_DIM = 128
KV_HEADS = 8
BLK = 64
SEL = 8
CAP = 2
QBD = 8
SEQS = 3
SEQ = 8192
NKB = 128
N_CTX = 16


def draw_lin_value(key, part):
    second_key = jax.random.fold_in(jax.random.fold_in(key, 5), 1)
    head_index = (jnp.arange(HEADS * HEAD_DIM) // HEAD_DIM).astype(jnp.float32)
    fraction = head_index / max(HEADS - 1, 1)
    shape_all = (SEQS, SEQ, HEADS * HEAD_DIM)
    base_vals = jnp.clip(jax.random.normal(second_key, shape_all, jnp.float32), -6.0, 6.0)
    return (base_vals * 3.0 ** fraction).astype(jnp.bfloat16)


def sparse_pair(key):
    base_key = jax.random.fold_in(key, 11)
    key_one, key_two = jax.random.split(base_key, 2)
    group_size = HEADS // KV_HEADS
    key_shape = (SEQS, SEQ, KV_HEADS, HEAD_DIM)
    query_vals = jnp.clip(jax.random.normal(key_two, (SEQS, SEQ, KV_HEADS, group_size, HEAD_DIM), jnp.float32), -6.0, 6.0)
    key_vals = jnp.clip(jax.random.normal(key_one, key_shape, jnp.float32), -4.0, 4.0)
    return (key_vals.reshape(SEQS, SEQ, KV_HEADS * HEAD_DIM), query_vals.reshape(SEQS, SEQ, HEADS * HEAD_DIM))


def draw_sparse_query(key, part):
    return sparse_pair(key)[1].astype(jnp.bfloat16)


def draw_sparse_key(key, part):
    return sparse_pair(key)[0].astype(jnp.bfloat16)


def draw_block_lists(key, part):
    ctx_count = NKB // QBD
    pool_size = ctx_count * CAP + QBD

    def one_sequence(seq_key):
        first_key, second_key = jax.random.split(seq_key)
        cand_scores = jax.random.randint(first_key, (ctx_count, ctx_count, QBD), 0, 1 << 20) * QBD + jnp.arange(QBD)
        chosen_local = lax.top_k(cand_scores, CAP)[1]
        remote_table = jnp.arange(ctx_count)[None, :, None] * QBD + chosen_local
        device_of = jnp.arange(NKB) // QBD
        local_of = jnp.arange(NKB) % QBD
        remote_blocks = remote_table[device_of].reshape(NKB, ctx_count * CAP)
        source_index = jnp.broadcast_to(jnp.arange(ctx_count)[None, :, None], (NKB, ctx_count, CAP))
        remote_valid = (source_index < device_of[:, None, None]).reshape(NKB, ctx_count * CAP)
        forced = ((local_of[:, None, None] == 0) & (source_index == device_of[:, None, None] - 1)).reshape(NKB, ctx_count * CAP)
        local_blocks = device_of[:, None] * QBD + jnp.arange(QBD)[None, :]
        local_valid = jnp.arange(QBD)[None, :] != local_of[:, None]
        candidates = jnp.concatenate([remote_blocks, local_blocks], axis=1)
        valid = jnp.concatenate([remote_valid, local_valid], axis=1).astype(jnp.int32)
        forced_all = jnp.concatenate([forced, jnp.zeros((NKB, QBD), bool)], axis=1).astype(jnp.int32)
        pick_scores = jax.random.randint(second_key, (NKB, pool_size), 0, 1 << 20) * pool_size + jnp.arange(pool_size)
        pick_scores = pick_scores + forced_all * (1 << 29) - (1 - valid) * (1 << 30)
        chosen = lax.top_k(pick_scores, SEL - 1)[1]
        picked = jnp.take_along_axis(candidates, chosen, axis=1)
        return jnp.concatenate([jnp.arange(NKB)[:, None], picked], axis=1).astype(jnp.int32)
    return jax.vmap(one_sequence)(jax.random.split(key, SEQS))


def shard_levels(key, extent, cuts, least, top_value):
    level = 1.0
    for axis_at, parts in cuts:
        heights = jax.random.uniform(jax.random.fold_in(jax.random.fold_in(key, 6), axis_at), (parts,), jnp.float32, least / len(cuts), top_value / len(cuts))
        level = level * jnp.repeat(jnp.exp(heights), extent[axis_at] // parts).reshape((-1,) + (1,) * (len(extent) - 1 - axis_at))
    return level


def bell_draw(stream_key, shape, deviation, reach, cuts=(), kind=jnp.bfloat16):
    drawn = deviation * jax.random.normal(stream_key, shape, jnp.float32)
    if cuts:
        drawn = drawn * shard_levels(stream_key, shape, cuts, -0.22, 0.18)
    return jnp.clip(drawn, -reach, reach).astype(kind)


def setup_inputs(seed: int = 0) -> dict:
    key_of = jax.random.split(jax.random.key(seed), 9)
    return {
        "lin_query": bell_draw(key_of[0], (SEQS, SEQ, HEADS * HEAD_DIM), 1.0, 6.0, ((1, 16), (2, 8))),
        "lin_key": bell_draw(key_of[1], (SEQS, SEQ, HEADS * HEAD_DIM), 1.0, 6.0, ((1, 16), (2, 8))),
        "lin_value": draw_lin_value(jax.random.fold_in(key_of[8], 71), 0),
        "lin_gain": jnp.clip(1.0 + 0.1 * jax.random.normal(key_of[3], (HEADS * HEAD_DIM,), jnp.float32), 0.5, 1.5),
        "sparse_query": draw_sparse_query(jax.random.fold_in(key_of[8], 71), 0),
        "sparse_key": draw_sparse_key(jax.random.fold_in(key_of[8], 71), 0),
        "sparse_value": bell_draw(key_of[6], (SEQS, SEQ, KV_HEADS * HEAD_DIM), 1.0, 6.0, ((1, 16), (2, 8))),
        "block_lists": draw_block_lists(jax.random.fold_in(key_of[8], 71), 0),
    }


norm_eps = 1e-05

def add_segment(carried, seg_state):
    return (carried + seg_state, carried)

def linear_layer(queries, key_rows, value_rows, gain):
    seg_len = QBD * BLK
    q_all = queries.reshape(N_CTX, seg_len, HEADS, HEAD_DIM)
    k_all = key_rows.reshape(N_CTX, seg_len, HEADS, HEAD_DIM)
    v_all = value_rows.reshape(N_CTX, seg_len, HEADS, HEAD_DIM)
    states = jnp.einsum('ajhd,ajhe->ahde', k_all.astype(jnp.float32), v_all.astype(jnp.float32))
    _, earlier = lax.scan(add_segment, jnp.zeros(states.shape[1:], jnp.float32), states)
    causal = jnp.arange(seg_len)[:, None] >= jnp.arange(seg_len)[None, :]

    def one_segment(seg_item):
        q_seg, k_seg, v_seg, prior_state = seg_item
        scores = jnp.einsum('ihd,jhd->hij', q_seg.astype(jnp.float32), k_seg.astype(jnp.float32))
        weights = jnp.where(causal[None], scores, 0.0).astype(jnp.bfloat16)
        weights = lax.optimization_barrier(weights).astype(jnp.float32)
        inside_terms = jnp.einsum('hij,jhd->ihd', weights, v_seg.astype(jnp.float32))
        rounded_state = lax.optimization_barrier(prior_state.astype(jnp.bfloat16)).astype(jnp.float32)
        carried = jnp.einsum('ihd,hde->ihe', q_seg.astype(jnp.float32), rounded_state)
        return inside_terms + carried
    combined = lax.map(one_segment, (q_all, k_all, v_all, earlier)).reshape(SEQ, HEADS * HEAD_DIM)
    mean_square = lax.optimization_barrier(jnp.sum(combined * combined, axis=1, keepdims=True)) / (HEADS * HEAD_DIM)
    return (combined * lax.rsqrt(mean_square + norm_eps) * gain).astype(jnp.bfloat16)

def sparse_layer(queries, key_rows, value_rows, lists):
    group_size = HEADS // KV_HEADS
    q_all = queries.reshape(NKB, BLK, KV_HEADS, group_size, HEAD_DIM)
    k_all = key_rows.reshape(NKB, BLK, KV_HEADS, HEAD_DIM)
    v_all = value_rows.reshape(NKB, BLK, KV_HEADS, HEAD_DIM)
    offsets = jnp.arange(BLK, dtype=jnp.int32)

    def one_block(block_item):
        q_block, listed, block_index = block_item
        listed = listed.astype(jnp.int32)
        k_sel = k_all[listed].reshape(SEL * BLK, KV_HEADS, HEAD_DIM)
        v_sel = v_all[listed].reshape(SEL * BLK, KV_HEADS, HEAD_DIM)
        scores = jnp.einsum('igkd,jgd->gkij', q_block.astype(jnp.float32), k_sel.astype(jnp.float32))
        scores = scores * (1.0 / math.sqrt(HEAD_DIM))
        q_pos = block_index * BLK + offsets
        k_pos = (listed[:, None] * BLK + offsets[None, :]).reshape(SEL * BLK)
        visible = k_pos[None, :] <= q_pos[:, None]
        scores = jnp.where(visible, scores, -jnp.inf)
        row_max = lax.optimization_barrier(jnp.max(scores, axis=-1, keepdims=True))
        expo = jnp.exp(scores - row_max)
        probs = (expo / lax.optimization_barrier(jnp.sum(expo, axis=-1, keepdims=True))).astype(jnp.bfloat16)
        probs = lax.optimization_barrier(probs).astype(jnp.float32)
        mixed = jnp.einsum('gkij,jgd->igkd', probs, v_sel.astype(jnp.float32))
        return mixed.reshape(BLK, HEADS * HEAD_DIM).astype(jnp.bfloat16)
    block_ids = jnp.arange(NKB, dtype=jnp.int32)
    return lax.map(one_block, (q_all, lists, block_ids)).reshape(SEQ, HEADS * HEAD_DIM)

def reference(lin_query, lin_key, lin_value, lin_gain, sparse_query, sparse_key, sparse_value, block_lists):
    lin_parts = []
    sparse_parts = []
    for seq_index in range(SEQS):
        lin_parts.append(linear_layer(lin_query[seq_index], lin_key[seq_index], lin_value[seq_index], lin_gain))
        sparse_parts.append(sparse_layer(sparse_query[seq_index], sparse_key[seq_index], sparse_value[seq_index], block_lists[seq_index]))
    return (jnp.stack(lin_parts), jnp.stack(sparse_parts))
```

```python
import math

import jax
import jax.numpy as jnp
from jax import lax
from jax.sharding import Mesh, PartitionSpec as P

HEADS = 64
HEAD_DIM = 128
BLK = 64
SEL = 8


norm_eps = 1e-05


def masked_lower_sum(stacked, pos):
    lower = jnp.arange(stacked.shape[0]) < pos
    return jnp.sum(jnp.where(lower.reshape((-1,) + (1,) * (stacked.ndim - 1)), stacked, 0.0), axis=0)


def earlier_states(states):
    y_pos = lax.axis_index("y")
    y_count = lax.axis_size("y")
    along_y = lax.all_gather(states, "y")
    within = masked_lower_sum(along_y, y_pos)
    group_total = jnp.sum(along_y, axis=0)
    rows = group_total.shape[2] // y_count
    part = lax.dynamic_slice_in_dim(group_total, y_pos * rows, rows, axis=2)
    along_z = lax.all_gather(part, "z")
    before_part = masked_lower_sum(along_z, lax.axis_index("z"))
    before = lax.all_gather(before_part, "y", axis=2, tiled=True)
    return before + within


def body(
    lin_query, lin_key, lin_value, lin_gain, sparse_query, sparse_key, sparse_value, block_lists
):
    seq_count, tok_count, lane_width = lin_query.shape
    heads_here = lane_width // HEAD_DIM
    ctx_pos = lax.axis_index("z") * lax.axis_size("y") + lax.axis_index("y")
    queries = lin_query.reshape(seq_count, tok_count, heads_here, HEAD_DIM)
    key_rows = lin_key.reshape(seq_count, tok_count, heads_here, HEAD_DIM)
    value_rows = lin_value.reshape(seq_count, tok_count, heads_here, HEAD_DIM)
    states = jnp.einsum("sjhd,sjhe->shde", key_rows, value_rows, preferred_element_type=jnp.float32)

    earlier = earlier_states(states)
    scores = jnp.einsum("sihd,sjhd->shij", queries, key_rows, preferred_element_type=jnp.float32)
    causal = jnp.arange(tok_count)[:, None] >= jnp.arange(tok_count)[None, :]
    weights = jnp.where(causal[None, None], scores, 0.0).astype(jnp.bfloat16)
    inside_terms = jnp.einsum(
        "shij,sjhd->sihd", weights, value_rows, preferred_element_type=jnp.float32
    )
    carried_terms = jnp.einsum(
        "sihd,shde->sihe", queries, earlier.astype(jnp.bfloat16), preferred_element_type=jnp.float32
    )
    combined = (inside_terms + carried_terms).reshape(seq_count, tok_count, lane_width)
    local_squares = jnp.sum(combined * combined, axis=2)
    whole_squares = lax.psum(local_squares, "head")
    inv_rms = lax.rsqrt(whole_squares / (HEADS * HEAD_DIM) + norm_eps)
    lin_out = (combined * inv_rms[:, :, None] * lin_gain).astype(jnp.bfloat16)
    kv_width = sparse_key.shape[2]
    kv_here = kv_width // HEAD_DIM
    group_size = heads_here // kv_here
    qblocks = tok_count // BLK
    key_blocks = sparse_key.reshape(seq_count, qblocks, BLK, kv_width)
    value_blocks = sparse_value.reshape(seq_count, qblocks, BLK, kv_width)
    key_store, value_store = (
        lax.all_gather(key_blocks, ("z", "y"), axis=1, tiled=True),
        lax.all_gather(value_blocks, ("z", "y"), axis=1, tiled=True),
    )
    gather_index = block_lists.reshape(seq_count, qblocks * SEL)[:, :, None, None]
    sel_keys = jnp.take_along_axis(key_store, gather_index, axis=1).reshape(
        seq_count, qblocks, SEL * BLK, kv_here, HEAD_DIM
    )
    sel_values = jnp.take_along_axis(value_store, gather_index, axis=1).reshape(
        seq_count, qblocks, SEL * BLK, kv_here, HEAD_DIM
    )
    block_queries = sparse_query.reshape(seq_count, qblocks, BLK, kv_here, group_size, HEAD_DIM)
    sparse_scores = jnp.einsum(
        "sbigkd,sbjgd->sbgkij", block_queries, sel_keys, preferred_element_type=jnp.float32
    )
    sparse_scores = sparse_scores * (1.0 / math.sqrt(HEAD_DIM))
    offsets = jnp.arange(BLK, dtype=jnp.int32)
    query_pos = ((ctx_pos * qblocks + jnp.arange(qblocks, dtype=jnp.int32)) * BLK)[
        :, None
    ] + offsets[None, :]
    key_pos = (block_lists[:, :, :, None] * BLK + offsets).reshape(seq_count, qblocks, SEL * BLK)
    visible = key_pos[:, :, None, None, None, :] <= query_pos[None, :, None, None, :, None]
    sparse_scores = jnp.where(visible, sparse_scores, -jnp.inf)
    row_max = jnp.max(sparse_scores, axis=-1, keepdims=True)
    expo = jnp.exp(sparse_scores - row_max)
    probs = (expo / jnp.sum(expo, axis=-1, keepdims=True)).astype(jnp.bfloat16)
    mixed = jnp.einsum(
        "sbgkij,sbjgd->sbigkd", probs, sel_values, preferred_element_type=jnp.float32
    )
    sparse_out = mixed.astype(jnp.bfloat16).reshape(seq_count, tok_count, lane_width)
    return (lin_out, sparse_out)


def solution(mesh):
    in_specs = (
        P(None, "ctx", "head"),
        P(None, "ctx", "head"),
        P(None, "ctx", "head"),
        P("head"),
        P(None, "ctx", "head"),
        P(None, "ctx", "head"),
        P(None, "ctx", "head"),
        P(None, "ctx", None),
    )
    out_specs = (P(None, "ctx", "head"), P(None, "ctx", "head"))
    n_ctx, n_head = mesh.devices.shape
    y_count = 4 if n_ctx % 4 == 0 else 1
    grid = Mesh(mesh.devices.reshape(n_ctx // y_count, y_count, n_head), ("z", "y", "head"))

    def split(spec):
        return P(*[("z", "y") if part == "ctx" else part for part in spec])

    return jax.shard_map(
        body,
        mesh=grid,
        in_specs=tuple(split(s) for s in in_specs),
        out_specs=tuple(split(s) for s in out_specs),
        check_vma=False,
    )
```

```python
import math

import jax
import jax.numpy as jnp
from jax import lax
from jax.sharding import Mesh, PartitionSpec as P

HEADS = 64
HEAD_DIM = 128
BLK = 64
SEL = 8
CAP = 2


norm_eps = 1e-05


def earlier_states(states):
    y_pos = lax.axis_index("y")
    y_count = lax.axis_size("y")
    z_count = lax.axis_size("z")
    seq_count, heads_here, rows, cols = states.shape
    part_rows = rows // y_count
    quarters = states.reshape(seq_count, heads_here, y_count, part_rows, cols)

    def quarter(array, index):
        return lax.dynamic_index_in_dim(array, index, axis=2, keepdims=False)

    def cyclic(x, shift):
        return lax.ppermute(x, "y", [(i, (i + shift) % y_count) for i in range(y_count)])

    held = [quarter(quarters, y_pos)]
    for shift in range(1, y_count):
        held.append(cyclic(quarter(quarters, (y_pos + shift) % y_count), shift))
    sources = [(y_pos - shift) % y_count for shift in range(y_count)]
    group_total = sum(held[1:], held[0])
    from_below = jnp.zeros_like(group_total)
    for shift in range(1, z_count):
        pairs = [(i, i + shift) for i in range(z_count - shift)]
        from_below = from_below + lax.ppermute(group_total, "z", pairs)
    finished = []
    for target in range(y_count):
        within = from_below
        for source, piece in zip(sources, held):
            within = within + jnp.where(source < target, piece, 0.0)
        finished.append(within.astype(jnp.bfloat16))
    stacked = jnp.stack(finished)
    returned = [lax.dynamic_index_in_dim(stacked, y_pos, axis=0, keepdims=False)]
    for shift in range(1, y_count):
        outgoing = lax.dynamic_index_in_dim(stacked, (y_pos + shift) % y_count, axis=0, keepdims=False)
        returned.append(cyclic(outgoing, shift))
    by_shift = jnp.stack(returned)
    order = (y_pos - jnp.arange(y_count)) % y_count
    by_quarter = jnp.take(by_shift, order, axis=0)
    return jnp.moveaxis(by_quarter, 0, 2).reshape(seq_count, heads_here, rows, cols)


def listed_blocks(sparse_key, sparse_value, block_lists, ctx_pos, ctx_count):
    seq_count, tok_count, kv_width = sparse_key.shape
    qblocks = tok_count // BLK
    kv_blocks = jnp.stack(
        [sparse_key.reshape(seq_count, qblocks, BLK, kv_width),
         sparse_value.reshape(seq_count, qblocks, BLK, kv_width)],
        axis=2,
    )
    all_lists = lax.all_gather(block_lists, ("z", "y"), axis=1, tiled=True)
    all_lists = all_lists.reshape(seq_count, ctx_count, qblocks * SEL)
    mine = ctx_pos * qblocks + jnp.arange(qblocks, dtype=jnp.int32)
    wanted = jnp.any(all_lists[:, :, :, None] == mine, axis=2)
    rank = jnp.cumsum(wanted.astype(jnp.int32), axis=-1)
    slot_block = jnp.stack(
        [jnp.argmax(wanted & (rank == slot + 1), axis=-1) for slot in range(CAP)], axis=-1
    ).astype(jnp.int32)
    receivers = jnp.minimum(ctx_pos + jnp.arange(1, ctx_count), ctx_count - 1)
    send_index = jnp.take(slot_block, receivers, axis=1).reshape(seq_count, (ctx_count - 1) * CAP)
    outgoing = jnp.take_along_axis(kv_blocks, send_index[:, :, None, None, None], axis=1)
    outgoing = outgoing.reshape(seq_count, ctx_count - 1, CAP, 2, BLK, kv_width)
    store = [kv_blocks]
    for shift in range(1, ctx_count):
        pairs = [(i, i + shift) for i in range(ctx_count - shift)]
        store.append(lax.ppermute(outgoing[:, shift - 1], ("z", "y"), pairs))
    store = jnp.concatenate(store, axis=1)
    own_lists = block_lists.reshape(seq_count, qblocks * SEL)
    listed_here = jnp.any(
        own_lists[:, :, None] == jnp.arange(ctx_count * qblocks, dtype=jnp.int32), axis=1
    ).reshape(seq_count, ctx_count, qblocks)
    own_rank = (jnp.cumsum(listed_here.astype(jnp.int32), axis=-1) - 1).reshape(seq_count, ctx_count * qblocks)
    slot = jnp.take_along_axis(own_rank, own_lists, axis=1)
    source = own_lists // qblocks
    local = own_lists % qblocks
    remote = qblocks + (ctx_pos - source - 1) * CAP + slot
    store_index = jnp.clip(jnp.where(source == ctx_pos, local, remote), 0, store.shape[1] - 1)
    picked = jnp.take_along_axis(store, store_index[:, :, None, None, None], axis=1)
    keys = picked[:, :, 0].reshape(seq_count, qblocks, SEL * BLK, kv_width)
    values = picked[:, :, 1].reshape(seq_count, qblocks, SEL * BLK, kv_width)
    return keys, values


def body(
    lin_query, lin_key, lin_value, lin_gain, sparse_query, sparse_key, sparse_value, block_lists
):
    seq_count, tok_count, lane_width = lin_query.shape
    heads_here = lane_width // HEAD_DIM
    ctx_pos = lax.axis_index("z") * lax.axis_size("y") + lax.axis_index("y")
    queries = lin_query.reshape(seq_count, tok_count, heads_here, HEAD_DIM)
    key_rows = lin_key.reshape(seq_count, tok_count, heads_here, HEAD_DIM)
    value_rows = lin_value.reshape(seq_count, tok_count, heads_here, HEAD_DIM)
    states = jnp.einsum("sjhd,sjhe->shde", key_rows, value_rows, preferred_element_type=jnp.float32)

    earlier = earlier_states(states)
    scores = jnp.einsum("sihd,sjhd->shij", queries, key_rows, preferred_element_type=jnp.float32)
    causal = jnp.arange(tok_count)[:, None] >= jnp.arange(tok_count)[None, :]
    weights = jnp.where(causal[None, None], scores, 0.0).astype(jnp.bfloat16)
    inside_terms = jnp.einsum(
        "shij,sjhd->sihd", weights, value_rows, preferred_element_type=jnp.float32
    )
    carried_terms = jnp.einsum(
        "sihd,shde->sihe", queries, earlier, preferred_element_type=jnp.float32
    )
    combined = (inside_terms + carried_terms).reshape(seq_count, tok_count, lane_width)
    local_squares = jnp.sum(combined * combined, axis=2)
    whole_squares = lax.psum(local_squares, "head")
    inv_rms = lax.rsqrt(whole_squares / (HEADS * HEAD_DIM) + norm_eps)
    lin_out = (combined * inv_rms[:, :, None] * lin_gain).astype(jnp.bfloat16)
    kv_width = sparse_key.shape[2]
    kv_here = kv_width // HEAD_DIM
    group_size = heads_here // kv_here
    qblocks = tok_count // BLK
    ctx_count = lax.axis_size("z") * lax.axis_size("y")
    sel_keys, sel_values = listed_blocks(sparse_key, sparse_value, block_lists, ctx_pos, ctx_count)
    sel_keys = sel_keys.reshape(seq_count, qblocks, SEL * BLK, kv_here, HEAD_DIM)
    sel_values = sel_values.reshape(seq_count, qblocks, SEL * BLK, kv_here, HEAD_DIM)
    block_queries = sparse_query.reshape(seq_count, qblocks, BLK, kv_here, group_size, HEAD_DIM)
    sparse_scores = jnp.einsum(
        "sbigkd,sbjgd->sbgkij", block_queries, sel_keys, preferred_element_type=jnp.float32
    )
    sparse_scores = sparse_scores * (1.0 / math.sqrt(HEAD_DIM))
    offsets = jnp.arange(BLK, dtype=jnp.int32)
    query_pos = ((ctx_pos * qblocks + jnp.arange(qblocks, dtype=jnp.int32)) * BLK)[
        :, None
    ] + offsets[None, :]
    key_pos = (block_lists[:, :, :, None] * BLK + offsets).reshape(seq_count, qblocks, SEL * BLK)
    visible = key_pos[:, :, None, None, None, :] <= query_pos[None, :, None, None, :, None]
    sparse_scores = jnp.where(visible, sparse_scores, -jnp.inf)
    row_max = jnp.max(sparse_scores, axis=-1, keepdims=True)
    expo = jnp.exp(sparse_scores - row_max)
    probs = (expo / jnp.sum(expo, axis=-1, keepdims=True)).astype(jnp.bfloat16)
    mixed = jnp.einsum(
        "sbgkij,sbjgd->sbigkd", probs, sel_values, preferred_element_type=jnp.float32
    )
    sparse_out = mixed.astype(jnp.bfloat16).reshape(seq_count, tok_count, lane_width)
    return (lin_out, sparse_out)


def solution(mesh):
    in_specs = (
        P(None, "ctx", "head"),
        P(None, "ctx", "head"),
        P(None, "ctx", "head"),
        P("head"),
        P(None, "ctx", "head"),
        P(None, "ctx", "head"),
        P(None, "ctx", "head"),
        P(None, "ctx", None),
    )
    out_specs = (P(None, "ctx", "head"), P(None, "ctx", "head"))
    n_ctx, n_head = mesh.devices.shape
    y_count = 4 if n_ctx % 4 == 0 else 1
    grid = Mesh(mesh.devices.reshape(n_ctx // y_count, y_count, n_head), ("z", "y", "head"))

    def split(spec):
        return P(*[("z", "y") if part == "ctx" else part for part in spec])

    return jax.shard_map(
        body,
        mesh=grid,
        in_specs=tuple(split(s) for s in in_specs),
        out_specs=tuple(split(s) for s in out_specs),
        check_vma=False,
    )
```

```python
import math

import jax
import jax.numpy as jnp
from jax import lax
from jax.experimental import pallas as pl
from jax.experimental.pallas import tpu as pltpu
from jax.sharding import Mesh, PartitionSpec as P

HEADS = 64
HEAD_DIM = 128
BLK = 64
SEL = 8
CAP = 2


norm_eps = 1e-05


def earlier_states(states):
    y_pos = lax.axis_index("y")
    y_count = lax.axis_size("y")
    z_count = lax.axis_size("z")
    seq_count, heads_here, rows, cols = states.shape
    part_rows = rows // y_count
    quarters = states.reshape(seq_count, heads_here, y_count, part_rows, cols)

    def quarter(array, index):
        return lax.dynamic_index_in_dim(array, index, axis=2, keepdims=False)

    def cyclic(x, shift):
        return lax.ppermute(x, "y", [(i, (i + shift) % y_count) for i in range(y_count)])

    held = [quarter(quarters, y_pos)]
    for shift in range(1, y_count):
        held.append(cyclic(quarter(quarters, (y_pos + shift) % y_count), shift))
    sources = [(y_pos - shift) % y_count for shift in range(y_count)]
    group_total = sum(held[1:], held[0])
    from_below = jnp.zeros_like(group_total)
    for shift in range(1, z_count):
        pairs = [(i, i + shift) for i in range(z_count - shift)]
        from_below = from_below + lax.ppermute(group_total, "z", pairs)
    finished = []
    for target in range(y_count):
        within = from_below
        for source, piece in zip(sources, held):
            within = within + jnp.where(source < target, piece, 0.0)
        finished.append(within.astype(jnp.bfloat16))
    stacked = jnp.stack(finished)
    returned = [lax.dynamic_index_in_dim(stacked, y_pos, axis=0, keepdims=False)]
    for shift in range(1, y_count):
        outgoing = lax.dynamic_index_in_dim(stacked, (y_pos + shift) % y_count, axis=0, keepdims=False)
        returned.append(cyclic(outgoing, shift))
    by_shift = jnp.stack(returned)
    order = (y_pos - jnp.arange(y_count)) % y_count
    by_quarter = jnp.take(by_shift, order, axis=0)
    return jnp.moveaxis(by_quarter, 0, 2).reshape(seq_count, heads_here, rows, cols)


def listed_blocks(sparse_key, sparse_value, block_lists, ctx_pos, ctx_count):
    seq_count, tok_count, kv_width = sparse_key.shape
    qblocks = tok_count // BLK
    kv_blocks = jnp.stack(
        [sparse_key.reshape(seq_count, qblocks, BLK, kv_width),
         sparse_value.reshape(seq_count, qblocks, BLK, kv_width)],
        axis=2,
    )
    all_lists = lax.all_gather(block_lists, ("z", "y"), axis=1, tiled=True)
    all_lists = all_lists.reshape(seq_count, ctx_count, qblocks * SEL)
    mine = ctx_pos * qblocks + jnp.arange(qblocks, dtype=jnp.int32)
    wanted = jnp.any(all_lists[:, :, :, None] == mine, axis=2)
    rank = jnp.cumsum(wanted.astype(jnp.int32), axis=-1)
    slot_block = jnp.stack(
        [jnp.argmax(wanted & (rank == slot + 1), axis=-1) for slot in range(CAP)], axis=-1
    ).astype(jnp.int32)
    receivers = jnp.minimum(ctx_pos + jnp.arange(1, ctx_count), ctx_count - 1)
    send_index = jnp.take(slot_block, receivers, axis=1).reshape(seq_count, (ctx_count - 1) * CAP)
    outgoing = jnp.take_along_axis(kv_blocks, send_index[:, :, None, None, None], axis=1)
    outgoing = outgoing.reshape(seq_count, ctx_count - 1, CAP, 2, BLK, kv_width)
    store = [kv_blocks]
    for shift in range(1, ctx_count):
        pairs = [(i, i + shift) for i in range(ctx_count - shift)]
        store.append(lax.ppermute(outgoing[:, shift - 1], ("z", "y"), pairs))
    store = jnp.concatenate(store, axis=1)
    own_lists = block_lists.reshape(seq_count, qblocks * SEL)
    listed_here = jnp.any(
        own_lists[:, :, None] == jnp.arange(ctx_count * qblocks, dtype=jnp.int32), axis=1
    ).reshape(seq_count, ctx_count, qblocks)
    own_rank = (jnp.cumsum(listed_here.astype(jnp.int32), axis=-1) - 1).reshape(seq_count, ctx_count * qblocks)
    slot = jnp.take_along_axis(own_rank, own_lists, axis=1)
    source = own_lists // qblocks
    local = own_lists % qblocks
    remote = qblocks + (ctx_pos - source - 1) * CAP + slot
    store_index = jnp.clip(jnp.where(source == ctx_pos, local, remote), 0, store.shape[1] - 1)
    return store, store_index.astype(jnp.int32)


def _dot(a, b, contract):
    return lax.dot_general(a, b, (contract, ((), ())), preferred_element_type=jnp.float32)


def linear_kernel(q_ref, k_ref, v_ref, e_ref, out_ref, sq_ref):
    head = pl.program_id(1)
    q = q_ref[0]
    scores = _dot(q, k_ref[0], ((1,), (1,)))
    rows = lax.broadcasted_iota(jnp.int32, scores.shape, 0)
    cols = lax.broadcasted_iota(jnp.int32, scores.shape, 1)
    weights = jnp.where(rows >= cols, scores, 0.0).astype(jnp.bfloat16)
    inside = _dot(weights, v_ref[0], ((1,), (0,)))
    carried = _dot(q, e_ref[0, 0], ((1,), (0,)))
    combined = inside + carried
    out_ref[0] = combined
    squares = jnp.sum(combined * combined, axis=1, keepdims=True)

    @pl.when(head == 0)
    def _():
        sq_ref[0] = squares

    @pl.when(head > 0)
    def _():
        sq_ref[0] = sq_ref[0] + squares


def linear_mix(lin_query, lin_key, lin_value, earlier):
    seq_count, tok_count, lane_width = lin_query.shape
    heads_here = lane_width // HEAD_DIM
    tile = pl.BlockSpec((1, tok_count, HEAD_DIM), lambda s, h: (s, 0, h))
    return pl.pallas_call(
        linear_kernel,
        grid=(seq_count, heads_here),
        in_specs=[tile, tile, tile, pl.BlockSpec((1, 1, HEAD_DIM, HEAD_DIM), lambda s, h: (s, h, 0, 0))],
        out_specs=[tile, pl.BlockSpec((1, tok_count, 1), lambda s, h: (s, 0, 0))],
        out_shape=[
            jax.ShapeDtypeStruct((seq_count, tok_count, lane_width), jnp.float32),
            jax.ShapeDtypeStruct((seq_count, tok_count, 1), jnp.float32),
        ],
        compiler_params=pltpu.CompilerParams(dimension_semantics=("parallel", "arbitrary")),
        cost_estimate=pl.CostEstimate(
            flops=2 * seq_count * heads_here * (2 * tok_count * tok_count + tok_count * HEAD_DIM) * HEAD_DIM,
            transcendentals=0,
            bytes_accessed=seq_count * tok_count * lane_width * (3 * 2 + 4),
        ),
    )(lin_query, lin_key, lin_value, earlier)


def sparse_kernel(index_ref, q_ref, *refs):
    block_refs = refs[:SEL]
    kpos_ref, qpos_ref, out_ref = refs[SEL:]
    keys = jnp.concatenate([r[0, 0, 0] for r in block_refs], axis=0)
    values = jnp.concatenate([r[0, 0, 1] for r in block_refs], axis=0)
    heads_here = q_ref.shape[2] // HEAD_DIM
    queries = jnp.concatenate(
        [q_ref[0, :, h * HEAD_DIM:(h + 1) * HEAD_DIM] for h in range(heads_here)], axis=0
    )
    scores = _dot(queries, keys, ((1,), (1,))) * (1.0 / math.sqrt(HEAD_DIM))
    visible = kpos_ref[0, 0] <= qpos_ref[0]
    visible = jnp.concatenate([visible] * heads_here, axis=0)
    scores = jnp.where(visible, scores, -jnp.inf)
    row_max = jnp.max(scores, axis=1, keepdims=True)
    expo = jnp.exp(scores - row_max)
    probs = (expo / jnp.sum(expo, axis=1, keepdims=True)).astype(jnp.bfloat16)
    mixed = _dot(probs, values, ((1,), (0,))).astype(out_ref.dtype)
    rows = q_ref.shape[1]
    for h in range(heads_here):
        out_ref[0, :, h * HEAD_DIM:(h + 1) * HEAD_DIM] = mixed[h * rows:(h + 1) * rows]


def sparse_attend(sparse_query, store, store_index, key_pos, query_pos):
    seq_count, tok_count, lane_width = sparse_query.shape
    qblocks = tok_count // BLK
    kv_width = store.shape[-1]

    def listed(j):
        return pl.BlockSpec(
            (1, 1, 2, BLK, kv_width), lambda s, b, idx: (s, idx[s, b * SEL + j], 0, 0, 0)
        )

    grid_spec = pltpu.PrefetchScalarGridSpec(
        num_scalar_prefetch=1,
        grid=(seq_count, qblocks),
        in_specs=[pl.BlockSpec((1, BLK, lane_width), lambda s, b, idx: (s, b, 0))]
        + [listed(j) for j in range(SEL)]
        + [
            pl.BlockSpec((1, 1, 1, SEL * BLK), lambda s, b, idx: (s, b, 0, 0)),
            pl.BlockSpec((1, BLK, 1), lambda s, b, idx: (b, 0, 0)),
        ],
        out_specs=pl.BlockSpec((1, BLK, lane_width), lambda s, b, idx: (s, b, 0)),
    )
    heads_here = lane_width // HEAD_DIM
    return pl.pallas_call(
        sparse_kernel,
        grid_spec=grid_spec,
        out_shape=jax.ShapeDtypeStruct(sparse_query.shape, sparse_query.dtype),
        compiler_params=pltpu.CompilerParams(dimension_semantics=("parallel", "parallel")),
        cost_estimate=pl.CostEstimate(
            flops=4 * seq_count * qblocks * heads_here * BLK * SEL * BLK * HEAD_DIM,
            transcendentals=seq_count * qblocks * heads_here * BLK * SEL * BLK,
            bytes_accessed=2 * 2 * seq_count * tok_count * lane_width + 4 * seq_count * qblocks * SEL * BLK * kv_width,
        ),
    )(store_index, sparse_query, *([store] * SEL), key_pos, query_pos)


def body(
    lin_query, lin_key, lin_value, lin_gain, sparse_query, sparse_key, sparse_value, block_lists
):
    seq_count, tok_count, lane_width = lin_query.shape
    heads_here = lane_width // HEAD_DIM
    ctx_pos = lax.axis_index("z") * lax.axis_size("y") + lax.axis_index("y")
    queries = lin_query.reshape(seq_count, tok_count, heads_here, HEAD_DIM)
    key_rows = lin_key.reshape(seq_count, tok_count, heads_here, HEAD_DIM)
    value_rows = lin_value.reshape(seq_count, tok_count, heads_here, HEAD_DIM)
    states = jnp.einsum("sjhd,sjhe->shde", key_rows, value_rows, preferred_element_type=jnp.float32)

    earlier = earlier_states(states)
    combined, row_squares = linear_mix(lin_query, lin_key, lin_value, earlier)
    local_squares = row_squares[:, :, 0]
    whole_squares = lax.psum(local_squares, "head")
    inv_rms = lax.rsqrt(whole_squares / (HEADS * HEAD_DIM) + norm_eps)
    lin_out = (combined * inv_rms[:, :, None] * lin_gain).astype(jnp.bfloat16)
    kv_width = sparse_key.shape[2]
    kv_here = kv_width // HEAD_DIM
    group_size = heads_here // kv_here
    qblocks = tok_count // BLK
    ctx_count = lax.axis_size("z") * lax.axis_size("y")
    store, store_index = listed_blocks(sparse_key, sparse_value, block_lists, ctx_pos, ctx_count)
    offsets = jnp.arange(BLK, dtype=jnp.int32)
    query_pos = ((ctx_pos * qblocks + jnp.arange(qblocks, dtype=jnp.int32)) * BLK)[:, None] + offsets[None, :]
    key_pos = (block_lists[:, :, :, None] * BLK + offsets).reshape(seq_count, qblocks, 1, SEL * BLK)
    sparse_out = sparse_attend(sparse_query, store, store_index, key_pos, query_pos[:, :, None])
    return (lin_out, sparse_out)


def solution(mesh):
    in_specs = (
        P(None, "ctx", "head"),
        P(None, "ctx", "head"),
        P(None, "ctx", "head"),
        P("head"),
        P(None, "ctx", "head"),
        P(None, "ctx", "head"),
        P(None, "ctx", "head"),
        P(None, "ctx", None),
    )
    out_specs = (P(None, "ctx", "head"), P(None, "ctx", "head"))
    n_ctx, n_head = mesh.devices.shape
    y_count = 4 if n_ctx % 4 == 0 else 1
    grid = Mesh(mesh.devices.reshape(n_ctx // y_count, y_count, n_head), ("z", "y", "head"))

    def split(spec):
        return P(*[("z", "y") if part == "ctx" else part for part in spec])

    return jax.shard_map(
        body,
        mesh=grid,
        in_specs=tuple(split(s) for s in in_specs),
        out_specs=tuple(split(s) for s in out_specs),
        check_vma=False,
    )
```

```python
import math

import jax
import jax.numpy as jnp
from jax import lax
from jax.experimental import pallas as pl
from jax.experimental.pallas import tpu as pltpu
from jax.sharding import Mesh, PartitionSpec as P

HEADS = 64
HEAD_DIM = 128
BLK = 64
SEL = 8
CAP = 2


norm_eps = 1e-05


def earlier_states(states):
    y_pos = lax.axis_index("y")
    y_count = lax.axis_size("y")
    z_count = lax.axis_size("z")
    seq_count, heads_here, rows, cols = states.shape
    part_rows = rows // y_count
    quarters = states.reshape(seq_count, heads_here, y_count, part_rows, cols)

    def quarter(array, index):
        return lax.dynamic_index_in_dim(array, index, axis=2, keepdims=False)

    def cyclic(x, shift):
        return lax.ppermute(x, "y", [(i, (i + shift) % y_count) for i in range(y_count)])

    held = [quarter(quarters, y_pos)]
    for shift in range(1, y_count):
        held.append(cyclic(quarter(quarters, (y_pos + shift) % y_count), shift))
    sources = [(y_pos - shift) % y_count for shift in range(y_count)]
    group_total = sum(held[1:], held[0])
    from_below = jnp.zeros_like(group_total)
    for shift in range(1, z_count):
        pairs = [(i, i + shift) for i in range(z_count - shift)]
        from_below = from_below + lax.ppermute(group_total, "z", pairs)
    finished = []
    for target in range(y_count):
        within = from_below
        for source, piece in zip(sources, held):
            within = within + jnp.where(source < target, piece, 0.0)
        finished.append(within.astype(jnp.bfloat16))
    stacked = jnp.stack(finished)
    returned = [lax.dynamic_index_in_dim(stacked, y_pos, axis=0, keepdims=False)]
    for shift in range(1, y_count):
        outgoing = lax.dynamic_index_in_dim(stacked, (y_pos + shift) % y_count, axis=0, keepdims=False)
        returned.append(cyclic(outgoing, shift))
    by_shift = jnp.stack(returned)
    order = (y_pos - jnp.arange(y_count)) % y_count
    by_quarter = jnp.take(by_shift, order, axis=0)
    return jnp.moveaxis(by_quarter, 0, 2).reshape(seq_count, heads_here, rows, cols)


def listed_blocks(sparse_key, sparse_value, block_lists, ctx_pos, ctx_count):
    seq_count, tok_count, kv_width = sparse_key.shape
    qblocks = tok_count // BLK
    kv_blocks = jnp.stack(
        [sparse_key.reshape(seq_count, qblocks, BLK, kv_width),
         sparse_value.reshape(seq_count, qblocks, BLK, kv_width)],
        axis=2,
    )
    own_lists = block_lists.reshape(seq_count, qblocks * SEL)
    listed_here = jnp.any(
        own_lists[:, :, None] == jnp.arange(ctx_count * qblocks, dtype=jnp.int32), axis=1
    ).reshape(seq_count, ctx_count, qblocks)
    rank = jnp.cumsum(listed_here.astype(jnp.int32), axis=-1)
    wanted = jnp.stack(
        [jnp.argmax(listed_here & (rank == slot + 1), axis=-1) for slot in range(CAP)], axis=-1
    ).astype(jnp.int32)
    requests = jnp.moveaxis(wanted, 1, 0)
    asked = lax.all_to_all(requests, ("z", "y"), 0, 0, tiled=True)
    send_index = (asked + jnp.arange(seq_count, dtype=jnp.int32)[None, :, None] * qblocks).reshape(-1)
    outgoing = jnp.take(kv_blocks.reshape(seq_count * qblocks, 2, BLK, kv_width), send_index, axis=0)
    arrived = lax.all_to_all(outgoing, ("z", "y"), 0, 0, tiled=True)
    store = jnp.concatenate(
        [kv_blocks.reshape(seq_count * qblocks, 2, BLK, kv_width), arrived], axis=0
    )
    own_rank = (rank - 1).reshape(seq_count, ctx_count * qblocks)
    slot = jnp.take_along_axis(own_rank, own_lists, axis=1)
    source = own_lists // qblocks
    local = own_lists % qblocks
    seq_ids = jnp.arange(seq_count, dtype=jnp.int32)[:, None]
    remote = seq_count * qblocks + (source * seq_count + seq_ids) * CAP + slot
    store_index = jnp.where(source == ctx_pos, seq_ids * qblocks + local, remote)
    store_index = jnp.clip(store_index, 0, store.shape[0] - 1)
    return store, store_index.astype(jnp.int32)


def _dot(a, b, contract):
    return lax.dot_general(a, b, (contract, ((), ())), preferred_element_type=jnp.float32)


def linear_kernel(q_ref, k_ref, v_ref, e_ref, out_ref, sq_ref):
    head = pl.program_id(1)
    q = q_ref[0]
    scores = _dot(q, k_ref[0], ((1,), (1,)))
    rows = lax.broadcasted_iota(jnp.int32, scores.shape, 0)
    cols = lax.broadcasted_iota(jnp.int32, scores.shape, 1)
    weights = jnp.where(rows >= cols, scores, 0.0).astype(jnp.bfloat16)
    inside = _dot(weights, v_ref[0], ((1,), (0,)))
    carried = _dot(q, e_ref[0, 0], ((1,), (0,)))
    combined = inside + carried
    out_ref[0] = combined
    squares = jnp.sum(combined * combined, axis=1, keepdims=True)

    @pl.when(head == 0)
    def _():
        sq_ref[0] = squares

    @pl.when(head > 0)
    def _():
        sq_ref[0] = sq_ref[0] + squares


def linear_mix(lin_query, lin_key, lin_value, earlier):
    seq_count, tok_count, lane_width = lin_query.shape
    heads_here = lane_width // HEAD_DIM
    tile = pl.BlockSpec((1, tok_count, HEAD_DIM), lambda s, h: (s, 0, h))
    return pl.pallas_call(
        linear_kernel,
        grid=(seq_count, heads_here),
        in_specs=[tile, tile, tile, pl.BlockSpec((1, 1, HEAD_DIM, HEAD_DIM), lambda s, h: (s, h, 0, 0))],
        out_specs=[tile, pl.BlockSpec((1, tok_count, 1), lambda s, h: (s, 0, 0))],
        out_shape=[
            jax.ShapeDtypeStruct((seq_count, tok_count, lane_width), jnp.float32),
            jax.ShapeDtypeStruct((seq_count, tok_count, 1), jnp.float32),
        ],
        compiler_params=pltpu.CompilerParams(dimension_semantics=("parallel", "arbitrary")),
        cost_estimate=pl.CostEstimate(
            flops=2 * seq_count * heads_here * (2 * tok_count * tok_count + tok_count * HEAD_DIM) * HEAD_DIM,
            transcendentals=0,
            bytes_accessed=seq_count * tok_count * lane_width * (3 * 2 + 4),
        ),
    )(lin_query, lin_key, lin_value, earlier)


def sparse_kernel(index_ref, q_ref, *refs):
    block_refs = refs[:SEL]
    kpos_ref, qpos_ref, out_ref = refs[SEL:]
    keys = jnp.concatenate([r[0, 0] for r in block_refs], axis=0)
    values = jnp.concatenate([r[0, 1] for r in block_refs], axis=0)
    heads_here = q_ref.shape[2] // HEAD_DIM
    queries = jnp.concatenate(
        [q_ref[0, :, h * HEAD_DIM:(h + 1) * HEAD_DIM] for h in range(heads_here)], axis=0
    )
    scores = _dot(queries, keys, ((1,), (1,))) * (1.0 / math.sqrt(HEAD_DIM))
    visible = kpos_ref[0, 0] <= qpos_ref[0]
    visible = jnp.concatenate([visible] * heads_here, axis=0)
    scores = jnp.where(visible, scores, -jnp.inf)
    row_max = jnp.max(scores, axis=1, keepdims=True)
    expo = jnp.exp(scores - row_max)
    probs = (expo / jnp.sum(expo, axis=1, keepdims=True)).astype(jnp.bfloat16)
    mixed = _dot(probs, values, ((1,), (0,))).astype(out_ref.dtype)
    rows = q_ref.shape[1]
    for h in range(heads_here):
        out_ref[0, :, h * HEAD_DIM:(h + 1) * HEAD_DIM] = mixed[h * rows:(h + 1) * rows]


def sparse_attend(sparse_query, store, store_index, key_pos, query_pos):
    seq_count, tok_count, lane_width = sparse_query.shape
    qblocks = tok_count // BLK
    kv_width = store.shape[-1]

    def listed(j):
        return pl.BlockSpec(
            (1, 2, BLK, kv_width), lambda s, b, idx: (idx[s, b * SEL + j], 0, 0, 0)
        )

    grid_spec = pltpu.PrefetchScalarGridSpec(
        num_scalar_prefetch=1,
        grid=(seq_count, qblocks),
        in_specs=[pl.BlockSpec((1, BLK, lane_width), lambda s, b, idx: (s, b, 0))]
        + [listed(j) for j in range(SEL)]
        + [
            pl.BlockSpec((1, 1, 1, SEL * BLK), lambda s, b, idx: (s, b, 0, 0)),
            pl.BlockSpec((1, BLK, 1), lambda s, b, idx: (b, 0, 0)),
        ],
        out_specs=pl.BlockSpec((1, BLK, lane_width), lambda s, b, idx: (s, b, 0)),
    )
    heads_here = lane_width // HEAD_DIM
    return pl.pallas_call(
        sparse_kernel,
        grid_spec=grid_spec,
        out_shape=jax.ShapeDtypeStruct(sparse_query.shape, sparse_query.dtype),
        compiler_params=pltpu.CompilerParams(dimension_semantics=("parallel", "parallel")),
        cost_estimate=pl.CostEstimate(
            flops=4 * seq_count * qblocks * heads_here * BLK * SEL * BLK * HEAD_DIM,
            transcendentals=seq_count * qblocks * heads_here * BLK * SEL * BLK,
            bytes_accessed=2 * 2 * seq_count * tok_count * lane_width + 4 * seq_count * qblocks * SEL * BLK * kv_width,
        ),
    )(store_index, sparse_query, *([store] * SEL), key_pos, query_pos)


def body(
    lin_query, lin_key, lin_value, lin_gain, sparse_query, sparse_key, sparse_value, block_lists
):
    seq_count, tok_count, lane_width = lin_query.shape
    heads_here = lane_width // HEAD_DIM
    ctx_pos = lax.axis_index("z") * lax.axis_size("y") + lax.axis_index("y")
    queries = lin_query.reshape(seq_count, tok_count, heads_here, HEAD_DIM)
    key_rows = lin_key.reshape(seq_count, tok_count, heads_here, HEAD_DIM)
    value_rows = lin_value.reshape(seq_count, tok_count, heads_here, HEAD_DIM)
    states = jnp.einsum("sjhd,sjhe->shde", key_rows, value_rows, preferred_element_type=jnp.float32)

    earlier = earlier_states(states)
    combined, row_squares = linear_mix(lin_query, lin_key, lin_value, earlier)
    local_squares = row_squares[:, :, 0]
    whole_squares = lax.psum(local_squares, "head")
    inv_rms = lax.rsqrt(whole_squares / (HEADS * HEAD_DIM) + norm_eps)
    lin_out = (combined * inv_rms[:, :, None] * lin_gain).astype(jnp.bfloat16)
    kv_width = sparse_key.shape[2]
    kv_here = kv_width // HEAD_DIM
    group_size = heads_here // kv_here
    qblocks = tok_count // BLK
    ctx_count = lax.axis_size("z") * lax.axis_size("y")
    store, store_index = listed_blocks(sparse_key, sparse_value, block_lists, ctx_pos, ctx_count)
    offsets = jnp.arange(BLK, dtype=jnp.int32)
    query_pos = ((ctx_pos * qblocks + jnp.arange(qblocks, dtype=jnp.int32)) * BLK)[:, None] + offsets[None, :]
    key_pos = (block_lists[:, :, :, None] * BLK + offsets).reshape(seq_count, qblocks, 1, SEL * BLK)
    sparse_out = sparse_attend(sparse_query, store, store_index, key_pos, query_pos[:, :, None])
    return (lin_out, sparse_out)


def solution(mesh):
    in_specs = (
        P(None, "ctx", "head"),
        P(None, "ctx", "head"),
        P(None, "ctx", "head"),
        P("head"),
        P(None, "ctx", "head"),
        P(None, "ctx", "head"),
        P(None, "ctx", "head"),
        P(None, "ctx", None),
    )
    out_specs = (P(None, "ctx", "head"), P(None, "ctx", "head"))
    n_ctx, n_head = mesh.devices.shape
    y_count = 4 if n_ctx % 4 == 0 else 1
    grid = Mesh(mesh.devices.reshape(n_ctx // y_count, y_count, n_head), ("z", "y", "head"))

    def split(spec):
        return P(*[("z", "y") if part == "ctx" else part for part in spec])

    return jax.shard_map(
        body,
        mesh=grid,
        in_specs=tuple(split(s) for s in in_specs),
        out_specs=tuple(split(s) for s in out_specs),
        check_vma=False,
    )
```

```python
import math

import jax
import jax.numpy as jnp
from jax import lax
from jax.experimental import pallas as pl
from jax.experimental.pallas import tpu as pltpu
from jax.sharding import Mesh, PartitionSpec as P

HEADS = 64
HEAD_DIM = 128
BLK = 64
SEL = 8
CAP = 2


norm_eps = 1e-05


def earlier_states(states, cover):
    y_pos = lax.axis_index("y")
    y_count = lax.axis_size("y")
    z_count = lax.axis_size("z")
    seq_count, heads_here, rows, cols = states.shape
    part_rows = rows // y_count
    quarters = states.reshape(seq_count, heads_here, y_count, part_rows, cols)

    def quarter(array, index):
        return lax.dynamic_index_in_dim(array, index, axis=2, keepdims=False)

    def cyclic(x, shift):
        return lax.ppermute(x, "y", [(i, (i + shift) % y_count) for i in range(y_count)])

    held = [quarter(quarters, y_pos)]
    for shift in range(1, y_count):
        held.append(cyclic(quarter(quarters, (y_pos + shift) % y_count), shift))
    sources = [(y_pos - shift) % y_count for shift in range(y_count)]
    group_total = sum(held[1:], held[0])
    below = []
    for shift in range(1, z_count):
        pairs = [(i, i + shift) for i in range(z_count - shift)]
        below.append(lax.ppermute(group_total, "z", pairs))
    below, covered = lax.optimization_barrier((below, cover))
    from_below = sum(below[1:], below[0])
    finished = []
    for target in range(y_count):
        within = from_below
        for source, piece in zip(sources, held):
            within = within + jnp.where(source < target, piece, 0.0)
        finished.append(within.astype(jnp.bfloat16))
    stacked = jnp.stack(finished)
    returned = [lax.dynamic_index_in_dim(stacked, y_pos, axis=0, keepdims=False)]
    for shift in range(1, y_count):
        outgoing = lax.dynamic_index_in_dim(stacked, (y_pos + shift) % y_count, axis=0, keepdims=False)
        returned.append(cyclic(outgoing, shift))
    by_shift = jnp.stack(returned)
    order = (y_pos - jnp.arange(y_count)) % y_count
    by_quarter = jnp.take(by_shift, order, axis=0)
    return jnp.moveaxis(by_quarter, 0, 2).reshape(seq_count, heads_here, rows, cols), covered


def listed_blocks(sparse_key, sparse_value, block_lists, ctx_pos, ctx_count):
    seq_count, tok_count, kv_width = sparse_key.shape
    qblocks = tok_count // BLK
    kv_blocks = jnp.stack(
        [sparse_key.reshape(seq_count, qblocks, BLK, kv_width),
         sparse_value.reshape(seq_count, qblocks, BLK, kv_width)],
        axis=2,
    )
    own_lists = block_lists.reshape(seq_count, qblocks * SEL)
    listed_here = jnp.any(
        own_lists[:, :, None] == jnp.arange(ctx_count * qblocks, dtype=jnp.int32), axis=1
    ).reshape(seq_count, ctx_count, qblocks)
    rank = jnp.cumsum(listed_here.astype(jnp.int32), axis=-1)
    wanted = jnp.stack(
        [jnp.argmax(listed_here & (rank == slot + 1), axis=-1) for slot in range(CAP)], axis=-1
    ).astype(jnp.int32)
    requests = jnp.moveaxis(wanted, 1, 0)
    asked = lax.all_to_all(requests, ("z", "y"), 0, 0, tiled=True)
    send_index = (asked + jnp.arange(seq_count, dtype=jnp.int32)[None, :, None] * qblocks).reshape(-1)
    outgoing = jnp.take(kv_blocks.reshape(seq_count * qblocks, 2, BLK, kv_width), send_index, axis=0)
    arrived = lax.all_to_all(outgoing, ("z", "y"), 0, 0, tiled=True)
    store = jnp.concatenate(
        [kv_blocks.reshape(seq_count * qblocks, 2, BLK, kv_width), arrived], axis=0
    )
    own_rank = (rank - 1).reshape(seq_count, ctx_count * qblocks)
    slot = jnp.take_along_axis(own_rank, own_lists, axis=1)
    source = own_lists // qblocks
    local = own_lists % qblocks
    seq_ids = jnp.arange(seq_count, dtype=jnp.int32)[:, None]
    remote = seq_count * qblocks + (source * seq_count + seq_ids) * CAP + slot
    store_index = jnp.where(source == ctx_pos, seq_ids * qblocks + local, remote)
    store_index = jnp.clip(store_index, 0, store.shape[0] - 1)
    return store, store_index.astype(jnp.int32)


def _dot(a, b, contract):
    return lax.dot_general(a, b, (contract, ((), ())), preferred_element_type=jnp.float32)


def inside_kernel(q_ref, k_ref, v_ref, out_ref):
    scores = _dot(q_ref[0], k_ref[0], ((1,), (1,)))
    rows = lax.broadcasted_iota(jnp.int32, scores.shape, 0)
    cols = lax.broadcasted_iota(jnp.int32, scores.shape, 1)
    weights = jnp.where(rows >= cols, scores, 0.0).astype(jnp.bfloat16)
    out_ref[0] = _dot(weights, v_ref[0], ((1,), (0,)))


def finish_kernel(inside_ref, q_ref, e_ref, out_ref, sq_ref):
    head = pl.program_id(1)
    combined = inside_ref[0] + _dot(q_ref[0], e_ref[0, 0], ((1,), (0,)))
    out_ref[0] = combined
    squares = jnp.sum(combined * combined, axis=1, keepdims=True)

    @pl.when(head == 0)
    def _():
        sq_ref[0] = squares

    @pl.when(head > 0)
    def _():
        sq_ref[0] = sq_ref[0] + squares


def linear_inside(lin_query, lin_key, lin_value):
    seq_count, tok_count, lane_width = lin_query.shape
    heads_here = lane_width // HEAD_DIM
    tile = pl.BlockSpec((1, tok_count, HEAD_DIM), lambda s, h: (s, 0, h))
    return pl.pallas_call(
        inside_kernel,
        grid=(seq_count, heads_here),
        in_specs=[tile, tile, tile],
        out_specs=tile,
        out_shape=jax.ShapeDtypeStruct((seq_count, tok_count, lane_width), jnp.float32),
        compiler_params=pltpu.CompilerParams(dimension_semantics=("parallel", "parallel")),
        cost_estimate=pl.CostEstimate(
            flops=4 * seq_count * heads_here * tok_count * tok_count * HEAD_DIM,
            transcendentals=0,
            bytes_accessed=seq_count * tok_count * lane_width * (3 * 2 + 4),
        ),
    )(lin_query, lin_key, lin_value)


def linear_finish(inside, lin_query, earlier):
    seq_count, tok_count, lane_width = lin_query.shape
    heads_here = lane_width // HEAD_DIM
    tile = pl.BlockSpec((1, tok_count, HEAD_DIM), lambda s, h: (s, 0, h))
    return pl.pallas_call(
        finish_kernel,
        grid=(seq_count, heads_here),
        in_specs=[tile, tile, pl.BlockSpec((1, 1, HEAD_DIM, HEAD_DIM), lambda s, h: (s, h, 0, 0))],
        out_specs=[tile, pl.BlockSpec((1, tok_count, 1), lambda s, h: (s, 0, 0))],
        out_shape=[
            jax.ShapeDtypeStruct((seq_count, tok_count, lane_width), jnp.float32),
            jax.ShapeDtypeStruct((seq_count, tok_count, 1), jnp.float32),
        ],
        compiler_params=pltpu.CompilerParams(dimension_semantics=("parallel", "arbitrary")),
        cost_estimate=pl.CostEstimate(
            flops=2 * seq_count * heads_here * tok_count * HEAD_DIM * HEAD_DIM,
            transcendentals=0,
            bytes_accessed=seq_count * tok_count * lane_width * (2 + 4 + 4),
        ),
    )(inside, lin_query, earlier)


def sparse_kernel(index_ref, q_ref, *refs):
    block_refs = refs[:SEL]
    kpos_ref, qpos_ref, out_ref = refs[SEL:]
    keys = jnp.concatenate([r[0, 0] for r in block_refs], axis=0)
    values = jnp.concatenate([r[0, 1] for r in block_refs], axis=0)
    heads_here = q_ref.shape[2] // HEAD_DIM
    queries = jnp.concatenate(
        [q_ref[0, :, h * HEAD_DIM:(h + 1) * HEAD_DIM] for h in range(heads_here)], axis=0
    )
    scores = _dot(queries, keys, ((1,), (1,))) * (1.0 / math.sqrt(HEAD_DIM))
    visible = kpos_ref[0, 0] <= qpos_ref[0]
    visible = jnp.concatenate([visible] * heads_here, axis=0)
    scores = jnp.where(visible, scores, -jnp.inf)
    row_max = jnp.max(scores, axis=1, keepdims=True)
    expo = jnp.exp(scores - row_max)
    probs = (expo / jnp.sum(expo, axis=1, keepdims=True)).astype(jnp.bfloat16)
    mixed = _dot(probs, values, ((1,), (0,))).astype(out_ref.dtype)
    rows = q_ref.shape[1]
    for h in range(heads_here):
        out_ref[0, :, h * HEAD_DIM:(h + 1) * HEAD_DIM] = mixed[h * rows:(h + 1) * rows]


def sparse_attend(sparse_query, store, store_index, key_pos, query_pos):
    seq_count, tok_count, lane_width = sparse_query.shape
    qblocks = tok_count // BLK
    kv_width = store.shape[-1]

    def listed(j):
        return pl.BlockSpec(
            (1, 2, BLK, kv_width), lambda s, b, idx: (idx[s, b * SEL + j], 0, 0, 0)
        )

    grid_spec = pltpu.PrefetchScalarGridSpec(
        num_scalar_prefetch=1,
        grid=(seq_count, qblocks),
        in_specs=[pl.BlockSpec((1, BLK, lane_width), lambda s, b, idx: (s, b, 0))]
        + [listed(j) for j in range(SEL)]
        + [
            pl.BlockSpec((1, 1, 1, SEL * BLK), lambda s, b, idx: (s, b, 0, 0)),
            pl.BlockSpec((1, BLK, 1), lambda s, b, idx: (b, 0, 0)),
        ],
        out_specs=pl.BlockSpec((1, BLK, lane_width), lambda s, b, idx: (s, b, 0)),
    )
    heads_here = lane_width // HEAD_DIM
    return pl.pallas_call(
        sparse_kernel,
        grid_spec=grid_spec,
        out_shape=jax.ShapeDtypeStruct(sparse_query.shape, sparse_query.dtype),
        compiler_params=pltpu.CompilerParams(dimension_semantics=("parallel", "parallel")),
        cost_estimate=pl.CostEstimate(
            flops=4 * seq_count * qblocks * heads_here * BLK * SEL * BLK * HEAD_DIM,
            transcendentals=seq_count * qblocks * heads_here * BLK * SEL * BLK,
            bytes_accessed=2 * 2 * seq_count * tok_count * lane_width + 4 * seq_count * qblocks * SEL * BLK * kv_width,
        ),
    )(store_index, sparse_query, *([store] * SEL), key_pos, query_pos)


def body(
    lin_query, lin_key, lin_value, lin_gain, sparse_query, sparse_key, sparse_value, block_lists
):
    seq_count, tok_count, lane_width = lin_query.shape
    heads_here = lane_width // HEAD_DIM
    ctx_pos = lax.axis_index("z") * lax.axis_size("y") + lax.axis_index("y")
    queries = lin_query.reshape(seq_count, tok_count, heads_here, HEAD_DIM)
    key_rows = lin_key.reshape(seq_count, tok_count, heads_here, HEAD_DIM)
    value_rows = lin_value.reshape(seq_count, tok_count, heads_here, HEAD_DIM)
    states = jnp.einsum("sjhd,sjhe->shde", key_rows, value_rows, preferred_element_type=jnp.float32)

    kv_width = sparse_key.shape[2]
    qblocks = tok_count // BLK
    ctx_count = lax.axis_size("z") * lax.axis_size("y")
    store, store_index = listed_blocks(sparse_key, sparse_value, block_lists, ctx_pos, ctx_count)
    offsets = jnp.arange(BLK, dtype=jnp.int32)
    query_pos = ((ctx_pos * qblocks + jnp.arange(qblocks, dtype=jnp.int32)) * BLK)[:, None] + offsets[None, :]
    key_pos = (block_lists[:, :, :, None] * BLK + offsets).reshape(seq_count, qblocks, 1, SEL * BLK)
    sparse_out = sparse_attend(sparse_query, store, store_index, key_pos, query_pos[:, :, None])
    inside = linear_inside(lin_query, lin_key, lin_value)
    earlier, (inside, sparse_out) = earlier_states(states, (inside, sparse_out))
    combined, row_squares = linear_finish(inside, lin_query, earlier)
    local_squares = row_squares[:, :, 0]
    whole_squares = lax.psum(local_squares, "head")
    inv_rms = lax.rsqrt(whole_squares / (HEADS * HEAD_DIM) + norm_eps)
    lin_out = (combined * inv_rms[:, :, None] * lin_gain).astype(jnp.bfloat16)
    return (lin_out, sparse_out)


def solution(mesh):
    in_specs = (
        P(None, "ctx", "head"),
        P(None, "ctx", "head"),
        P(None, "ctx", "head"),
        P("head"),
        P(None, "ctx", "head"),
        P(None, "ctx", "head"),
        P(None, "ctx", "head"),
        P(None, "ctx", None),
    )
    out_specs = (P(None, "ctx", "head"), P(None, "ctx", "head"))
    n_ctx, n_head = mesh.devices.shape
    y_count = 4 if n_ctx % 4 == 0 else 1
    grid = Mesh(mesh.devices.reshape(n_ctx // y_count, y_count, n_head), ("z", "y", "head"))

    def split(spec):
        return P(*[("z", "y") if part == "ctx" else part for part in spec])

    return jax.shard_map(
        body,
        mesh=grid,
        in_specs=tuple(split(s) for s in in_specs),
        out_specs=tuple(split(s) for s in out_specs),
        check_vma=False,
    )
```

```python
import math

import jax
import jax.numpy as jnp
from jax import lax
from jax.experimental import pallas as pl
from jax.experimental.pallas import tpu as pltpu
from jax.sharding import Mesh, PartitionSpec as P

HEADS = 64
HEAD_DIM = 128
BLK = 64
SEL = 8
CAP = 2


norm_eps = 1e-05


def earlier_states(states, cover):
    y_pos = lax.axis_index("y")
    y_count = lax.axis_size("y")
    z_count = lax.axis_size("z")
    seq_count, heads_here, rows, cols = states.shape
    part_rows = rows // y_count
    quarters = states.reshape(seq_count, heads_here, y_count, part_rows, cols)

    def quarter(array, index):
        return lax.dynamic_index_in_dim(array, index, axis=2, keepdims=False)

    def cyclic(x, shift):
        return lax.ppermute(x, "y", [(i, (i + shift) % y_count) for i in range(y_count)])

    held = [quarter(quarters, y_pos)]
    for shift in range(1, y_count):
        held.append(cyclic(quarter(quarters, (y_pos + shift) % y_count), shift))
    sources = [(y_pos - shift) % y_count for shift in range(y_count)]
    group_total = sum(held[1:], held[0])
    below = []
    for shift in range(1, z_count):
        pairs = [(i, i + shift) for i in range(z_count - shift)]
        below.append(lax.ppermute(group_total, "z", pairs))
    below, covered = lax.optimization_barrier((below, cover))
    from_below = sum(below[1:], below[0])
    finished = []
    for target in range(y_count):
        within = from_below
        for source, piece in zip(sources, held):
            within = within + jnp.where(source < target, piece, 0.0)
        finished.append(within.astype(jnp.bfloat16))
    stacked = jnp.stack(finished)
    returned = [lax.dynamic_index_in_dim(stacked, y_pos, axis=0, keepdims=False)]
    for shift in range(1, y_count):
        outgoing = lax.dynamic_index_in_dim(stacked, (y_pos + shift) % y_count, axis=0, keepdims=False)
        returned.append(cyclic(outgoing, shift))
    by_shift = jnp.stack(returned)
    order = (y_pos - jnp.arange(y_count)) % y_count
    by_quarter = jnp.take(by_shift, order, axis=0)
    return jnp.moveaxis(by_quarter, 0, 2).reshape(seq_count, heads_here, rows, cols), covered


def listed_blocks(sparse_key, sparse_value, block_lists, ctx_pos, ctx_count):
    seq_count, tok_count, kv_width = sparse_key.shape
    qblocks = tok_count // BLK
    kv_blocks = jnp.stack(
        [sparse_key.reshape(seq_count, qblocks, BLK, kv_width),
         sparse_value.reshape(seq_count, qblocks, BLK, kv_width)],
        axis=2,
    )
    own_lists = block_lists.reshape(seq_count, qblocks * SEL)
    listed_here = jnp.any(
        own_lists[:, :, None] == jnp.arange(ctx_count * qblocks, dtype=jnp.int32), axis=1
    ).reshape(seq_count, ctx_count, qblocks)
    rank = jnp.cumsum(listed_here.astype(jnp.int32), axis=-1)
    wanted = jnp.stack(
        [jnp.argmax(listed_here & (rank == slot + 1), axis=-1) for slot in range(CAP)], axis=-1
    ).astype(jnp.int32)
    requests = jnp.moveaxis(wanted, 1, 0)
    asked = lax.all_to_all(requests, ("z", "y"), 0, 0, tiled=True)
    send_index = (asked + jnp.arange(seq_count, dtype=jnp.int32)[None, :, None] * qblocks).reshape(-1)
    outgoing = jnp.take(kv_blocks.reshape(seq_count * qblocks, 2, BLK, kv_width), send_index, axis=0)
    arrived = lax.all_to_all(outgoing, ("z", "y"), 0, 0, tiled=True)
    store = jnp.concatenate(
        [kv_blocks.reshape(seq_count * qblocks, 2, BLK, kv_width), arrived], axis=0
    )
    own_rank = (rank - 1).reshape(seq_count, ctx_count * qblocks)
    slot = jnp.take_along_axis(own_rank, own_lists, axis=1)
    source = own_lists // qblocks
    local = own_lists % qblocks
    seq_ids = jnp.arange(seq_count, dtype=jnp.int32)[:, None]
    remote = seq_count * qblocks + (source * seq_count + seq_ids) * CAP + slot
    store_index = jnp.where(source == ctx_pos, seq_ids * qblocks + local, remote)
    store_index = jnp.clip(store_index, 0, store.shape[0] - 1)
    return store, store_index.astype(jnp.int32)


def _dot(a, b, contract):
    return lax.dot_general(a, b, (contract, ((), ())), preferred_element_type=jnp.float32)


def inside_kernel(q_ref, k_ref, v_ref, out_ref):
    scores = _dot(q_ref[0], k_ref[0], ((1,), (1,)))
    rows = lax.broadcasted_iota(jnp.int32, scores.shape, 0)
    cols = lax.broadcasted_iota(jnp.int32, scores.shape, 1)
    weights = jnp.where(rows >= cols, scores, 0.0).astype(jnp.bfloat16)
    out_ref[0] = _dot(weights, v_ref[0], ((1,), (0,)))


def finish_kernel(inside_ref, q_ref, e_ref, out_ref, sq_ref):
    heads_here = e_ref.shape[1]
    total = None
    for h in range(heads_here):
        lanes = slice(h * HEAD_DIM, (h + 1) * HEAD_DIM)
        combined = inside_ref[0, :, lanes] + _dot(q_ref[0, :, lanes], e_ref[0, h], ((1,), (0,)))
        out_ref[0, :, lanes] = combined
        squares = jnp.sum(combined * combined, axis=1, keepdims=True)
        total = squares if total is None else total + squares
    sq_ref[0] = total


def linear_inside(lin_query, lin_key, lin_value):
    seq_count, tok_count, lane_width = lin_query.shape
    heads_here = lane_width // HEAD_DIM
    tile = pl.BlockSpec((1, tok_count, HEAD_DIM), lambda s, h: (s, 0, h))
    return pl.pallas_call(
        inside_kernel,
        grid=(seq_count, heads_here),
        in_specs=[tile, tile, tile],
        out_specs=tile,
        out_shape=jax.ShapeDtypeStruct((seq_count, tok_count, lane_width), jnp.float32),
        compiler_params=pltpu.CompilerParams(dimension_semantics=("parallel", "parallel")),
        cost_estimate=pl.CostEstimate(
            flops=4 * seq_count * heads_here * tok_count * tok_count * HEAD_DIM,
            transcendentals=0,
            bytes_accessed=seq_count * tok_count * lane_width * (3 * 2 + 4),
        ),
    )(lin_query, lin_key, lin_value)


def linear_finish(inside, lin_query, earlier):
    seq_count, tok_count, lane_width = lin_query.shape
    heads_here = lane_width // HEAD_DIM
    rows = pl.BlockSpec((1, tok_count, lane_width), lambda s: (s, 0, 0))
    return pl.pallas_call(
        finish_kernel,
        grid=(seq_count,),
        in_specs=[rows, rows, pl.BlockSpec((1, heads_here, HEAD_DIM, HEAD_DIM), lambda s: (s, 0, 0, 0))],
        out_specs=[rows, pl.BlockSpec((1, tok_count, 1), lambda s: (s, 0, 0))],
        out_shape=[
            jax.ShapeDtypeStruct((seq_count, tok_count, lane_width), jnp.float32),
            jax.ShapeDtypeStruct((seq_count, tok_count, 1), jnp.float32),
        ],
        compiler_params=pltpu.CompilerParams(dimension_semantics=("parallel",)),
        cost_estimate=pl.CostEstimate(
            flops=2 * seq_count * heads_here * tok_count * HEAD_DIM * HEAD_DIM,
            transcendentals=0,
            bytes_accessed=seq_count * tok_count * lane_width * (2 + 4 + 4),
        ),
    )(inside, lin_query, earlier)


def sparse_kernel(index_ref, q_ref, *refs):
    block_refs = refs[:SEL]
    kpos_ref, qpos_ref, out_ref = refs[SEL:]
    keys = jnp.concatenate([r[0, 0] for r in block_refs], axis=0)
    values = jnp.concatenate([r[0, 1] for r in block_refs], axis=0)
    heads_here = q_ref.shape[2] // HEAD_DIM
    queries = jnp.concatenate(
        [q_ref[0, :, h * HEAD_DIM:(h + 1) * HEAD_DIM] for h in range(heads_here)], axis=0
    )
    scores = _dot(queries, keys, ((1,), (1,))) * (1.0 / math.sqrt(HEAD_DIM))
    visible = kpos_ref[0, 0] <= qpos_ref[0]
    visible = jnp.concatenate([visible] * heads_here, axis=0)
    scores = jnp.where(visible, scores, -jnp.inf)
    row_max = jnp.max(scores, axis=1, keepdims=True)
    expo = jnp.exp(scores - row_max)
    probs = (expo / jnp.sum(expo, axis=1, keepdims=True)).astype(jnp.bfloat16)
    mixed = _dot(probs, values, ((1,), (0,))).astype(out_ref.dtype)
    rows = q_ref.shape[1]
    for h in range(heads_here):
        out_ref[0, :, h * HEAD_DIM:(h + 1) * HEAD_DIM] = mixed[h * rows:(h + 1) * rows]


def sparse_attend(sparse_query, store, store_index, key_pos, query_pos):
    seq_count, tok_count, lane_width = sparse_query.shape
    qblocks = tok_count // BLK
    kv_width = store.shape[-1]

    def listed(j):
        return pl.BlockSpec(
            (1, 2, BLK, kv_width), lambda s, b, idx: (idx[s, b * SEL + j], 0, 0, 0)
        )

    grid_spec = pltpu.PrefetchScalarGridSpec(
        num_scalar_prefetch=1,
        grid=(seq_count, qblocks),
        in_specs=[pl.BlockSpec((1, BLK, lane_width), lambda s, b, idx: (s, b, 0))]
        + [listed(j) for j in range(SEL)]
        + [
            pl.BlockSpec((1, 1, 1, SEL * BLK), lambda s, b, idx: (s, b, 0, 0)),
            pl.BlockSpec((1, BLK, 1), lambda s, b, idx: (b, 0, 0)),
        ],
        out_specs=pl.BlockSpec((1, BLK, lane_width), lambda s, b, idx: (s, b, 0)),
    )
    heads_here = lane_width // HEAD_DIM
    return pl.pallas_call(
        sparse_kernel,
        grid_spec=grid_spec,
        out_shape=jax.ShapeDtypeStruct(sparse_query.shape, sparse_query.dtype),
        compiler_params=pltpu.CompilerParams(dimension_semantics=("parallel", "parallel")),
        cost_estimate=pl.CostEstimate(
            flops=4 * seq_count * qblocks * heads_here * BLK * SEL * BLK * HEAD_DIM,
            transcendentals=seq_count * qblocks * heads_here * BLK * SEL * BLK,
            bytes_accessed=2 * 2 * seq_count * tok_count * lane_width + 4 * seq_count * qblocks * SEL * BLK * kv_width,
        ),
    )(store_index, sparse_query, *([store] * SEL), key_pos, query_pos)


def body(
    lin_query, lin_key, lin_value, lin_gain, sparse_query, sparse_key, sparse_value, block_lists
):
    seq_count, tok_count, lane_width = lin_query.shape
    heads_here = lane_width // HEAD_DIM
    ctx_pos = lax.axis_index("z") * lax.axis_size("y") + lax.axis_index("y")
    queries = lin_query.reshape(seq_count, tok_count, heads_here, HEAD_DIM)
    key_rows = lin_key.reshape(seq_count, tok_count, heads_here, HEAD_DIM)
    value_rows = lin_value.reshape(seq_count, tok_count, heads_here, HEAD_DIM)
    states = jnp.einsum("sjhd,sjhe->shde", key_rows, value_rows, preferred_element_type=jnp.float32)
    states, block_lists = lax.optimization_barrier((states, block_lists))

    kv_width = sparse_key.shape[2]
    qblocks = tok_count // BLK
    ctx_count = lax.axis_size("z") * lax.axis_size("y")
    store, store_index = listed_blocks(sparse_key, sparse_value, block_lists, ctx_pos, ctx_count)
    offsets = jnp.arange(BLK, dtype=jnp.int32)
    query_pos = ((ctx_pos * qblocks + jnp.arange(qblocks, dtype=jnp.int32)) * BLK)[:, None] + offsets[None, :]
    key_pos = (block_lists[:, :, :, None] * BLK + offsets).reshape(seq_count, qblocks, 1, SEL * BLK)
    sparse_out = sparse_attend(sparse_query, store, store_index, key_pos, query_pos[:, :, None])
    inside = linear_inside(lin_query, lin_key, lin_value)
    earlier, (inside, sparse_out) = earlier_states(states, (inside, sparse_out))
    combined, row_squares = linear_finish(inside, lin_query, earlier)
    local_squares = row_squares[:, :, 0]
    whole_squares = lax.psum(local_squares, "head")
    inv_rms = lax.rsqrt(whole_squares / (HEADS * HEAD_DIM) + norm_eps)
    lin_out = (combined * inv_rms[:, :, None] * lin_gain).astype(jnp.bfloat16)
    return (lin_out, sparse_out)


def solution(mesh):
    in_specs = (
        P(None, "ctx", "head"),
        P(None, "ctx", "head"),
        P(None, "ctx", "head"),
        P("head"),
        P(None, "ctx", "head"),
        P(None, "ctx", "head"),
        P(None, "ctx", "head"),
        P(None, "ctx", None),
    )
    out_specs = (P(None, "ctx", "head"), P(None, "ctx", "head"))
    n_ctx, n_head = mesh.devices.shape
    y_count = 4 if n_ctx % 4 == 0 else 1
    grid = Mesh(mesh.devices.reshape(n_ctx // y_count, y_count, n_head), ("z", "y", "head"))

    def split(spec):
        return P(*[("z", "y") if part == "ctx" else part for part in spec])

    return jax.shard_map(
        body,
        mesh=grid,
        in_specs=tuple(split(s) for s in in_specs),
        out_specs=tuple(split(s) for s in out_specs),
        check_vma=False,
    )
```

```python
import math

import jax
import jax.numpy as jnp
from jax import lax
from jax.experimental import pallas as pl
from jax.experimental.pallas import tpu as pltpu
from jax.sharding import Mesh, PartitionSpec as P

HEADS = 64
HEAD_DIM = 128
BLK = 64
SEL = 8
CAP = 2


norm_eps = 1e-05


def earlier_states(states, cover):
    y_pos = lax.axis_index("y")
    y_count = lax.axis_size("y")
    z_count = lax.axis_size("z")
    seq_count, heads_here, rows, cols = states.shape
    part_rows = rows // y_count
    quarters = states.reshape(seq_count, heads_here, y_count, part_rows, cols)

    def quarter(array, index):
        return lax.dynamic_index_in_dim(array, index, axis=2, keepdims=False)

    def cyclic(x, shift):
        return lax.ppermute(x, "y", [(i, (i + shift) % y_count) for i in range(y_count)])

    held = [quarter(quarters, y_pos)]
    for shift in range(1, y_count):
        held.append(cyclic(quarter(quarters, (y_pos + shift) % y_count), shift))
    held, covered = lax.optimization_barrier((held, cover))
    sources = [(y_pos - shift) % y_count for shift in range(y_count)]
    group_total = sum(held[1:], held[0])
    below = []
    for shift in range(1, z_count):
        pairs = [(i, i + shift) for i in range(z_count - shift)]
        below.append(lax.ppermute(group_total, "z", pairs))
    from_below = sum(below[1:], below[0])
    finished = []
    for target in range(y_count):
        within = from_below
        for source, piece in zip(sources, held):
            within = within + jnp.where(source < target, piece, 0.0)
        finished.append(within.astype(jnp.bfloat16))
    stacked = jnp.stack(finished)
    returned = [lax.dynamic_index_in_dim(stacked, y_pos, axis=0, keepdims=False)]
    for shift in range(1, y_count):
        outgoing = lax.dynamic_index_in_dim(stacked, (y_pos + shift) % y_count, axis=0, keepdims=False)
        returned.append(cyclic(outgoing, shift))
    by_shift = jnp.stack(returned)
    order = (y_pos - jnp.arange(y_count)) % y_count
    by_quarter = jnp.take(by_shift, order, axis=0)
    return jnp.moveaxis(by_quarter, 0, 2).reshape(seq_count, heads_here, rows, cols), covered


def listed_blocks(sparse_key, sparse_value, block_lists, ctx_pos, ctx_count):
    seq_count, tok_count, kv_width = sparse_key.shape
    qblocks = tok_count // BLK
    kv_blocks = jnp.stack(
        [sparse_key.reshape(seq_count, qblocks, BLK, kv_width),
         sparse_value.reshape(seq_count, qblocks, BLK, kv_width)],
        axis=2,
    )
    own_lists = block_lists.reshape(seq_count, qblocks * SEL)
    listed_here = jnp.any(
        own_lists[:, :, None] == jnp.arange(ctx_count * qblocks, dtype=jnp.int32), axis=1
    ).reshape(seq_count, ctx_count, qblocks)
    rank = jnp.cumsum(listed_here.astype(jnp.int32), axis=-1)
    wanted = jnp.stack(
        [jnp.argmax(listed_here & (rank == slot + 1), axis=-1) for slot in range(CAP)], axis=-1
    ).astype(jnp.int32)
    requests = jnp.moveaxis(wanted, 1, 0)
    asked = lax.all_to_all(requests, ("z", "y"), 0, 0, tiled=True)
    send_index = (asked + jnp.arange(seq_count, dtype=jnp.int32)[None, :, None] * qblocks).reshape(-1)
    outgoing = jnp.take(kv_blocks.reshape(seq_count * qblocks, 2, BLK, kv_width), send_index, axis=0)
    arrived = lax.all_to_all(outgoing, ("z", "y"), 0, 0, tiled=True)
    store = jnp.concatenate(
        [kv_blocks.reshape(seq_count * qblocks, 2, BLK, kv_width), arrived], axis=0
    )
    own_rank = (rank - 1).reshape(seq_count, ctx_count * qblocks)
    slot = jnp.take_along_axis(own_rank, own_lists, axis=1)
    source = own_lists // qblocks
    local = own_lists % qblocks
    seq_ids = jnp.arange(seq_count, dtype=jnp.int32)[:, None]
    remote = seq_count * qblocks + (source * seq_count + seq_ids) * CAP + slot
    store_index = jnp.where(source == ctx_pos, seq_ids * qblocks + local, remote)
    store_index = jnp.clip(store_index, 0, store.shape[0] - 1)
    return store, store_index.astype(jnp.int32)


def _dot(a, b, contract):
    return lax.dot_general(a, b, (contract, ((), ())), preferred_element_type=jnp.float32)


def inside_kernel(q_ref, k_ref, v_ref, out_ref):
    scores = _dot(q_ref[0], k_ref[0], ((1,), (1,)))
    rows = lax.broadcasted_iota(jnp.int32, scores.shape, 0)
    cols = lax.broadcasted_iota(jnp.int32, scores.shape, 1)
    weights = jnp.where(rows >= cols, scores, 0.0).astype(jnp.bfloat16)
    out_ref[0] = _dot(weights, v_ref[0], ((1,), (0,)))


def finish_kernel(inside_ref, q_ref, e_ref, out_ref, sq_ref):
    heads_here = e_ref.shape[1]
    total = None
    for h in range(heads_here):
        lanes = slice(h * HEAD_DIM, (h + 1) * HEAD_DIM)
        combined = inside_ref[0, :, lanes] + _dot(q_ref[0, :, lanes], e_ref[0, h], ((1,), (0,)))
        out_ref[0, :, lanes] = combined
        squares = jnp.sum(combined * combined, axis=1, keepdims=True)
        total = squares if total is None else total + squares
    sq_ref[0] = total


def linear_inside(lin_query, lin_key, lin_value):
    seq_count, tok_count, lane_width = lin_query.shape
    heads_here = lane_width // HEAD_DIM
    tile = pl.BlockSpec((1, tok_count, HEAD_DIM), lambda s, h: (s, 0, h))
    return pl.pallas_call(
        inside_kernel,
        grid=(seq_count, heads_here),
        in_specs=[tile, tile, tile],
        out_specs=tile,
        out_shape=jax.ShapeDtypeStruct((seq_count, tok_count, lane_width), jnp.float32),
        compiler_params=pltpu.CompilerParams(dimension_semantics=("parallel", "parallel")),
        cost_estimate=pl.CostEstimate(
            flops=4 * seq_count * heads_here * tok_count * tok_count * HEAD_DIM,
            transcendentals=0,
            bytes_accessed=seq_count * tok_count * lane_width * (3 * 2 + 4),
        ),
    )(lin_query, lin_key, lin_value)


def linear_finish(inside, lin_query, earlier):
    seq_count, tok_count, lane_width = lin_query.shape
    heads_here = lane_width // HEAD_DIM
    rows = pl.BlockSpec((1, tok_count, lane_width), lambda s: (s, 0, 0))
    return pl.pallas_call(
        finish_kernel,
        grid=(seq_count,),
        in_specs=[rows, rows, pl.BlockSpec((1, heads_here, HEAD_DIM, HEAD_DIM), lambda s: (s, 0, 0, 0))],
        out_specs=[rows, pl.BlockSpec((1, tok_count, 1), lambda s: (s, 0, 0))],
        out_shape=[
            jax.ShapeDtypeStruct((seq_count, tok_count, lane_width), jnp.float32),
            jax.ShapeDtypeStruct((seq_count, tok_count, 1), jnp.float32),
        ],
        compiler_params=pltpu.CompilerParams(dimension_semantics=("parallel",)),
        cost_estimate=pl.CostEstimate(
            flops=2 * seq_count * heads_here * tok_count * HEAD_DIM * HEAD_DIM,
            transcendentals=0,
            bytes_accessed=seq_count * tok_count * lane_width * (2 + 4 + 4),
        ),
    )(inside, lin_query, earlier)


def sparse_kernel(index_ref, q_ref, *refs):
    block_refs = refs[:SEL]
    kpos_ref, qpos_ref, out_ref = refs[SEL:]
    keys = jnp.concatenate([r[0, 0] for r in block_refs], axis=0)
    values = jnp.concatenate([r[0, 1] for r in block_refs], axis=0)
    heads_here = q_ref.shape[2] // HEAD_DIM
    queries = jnp.concatenate(
        [q_ref[0, :, h * HEAD_DIM:(h + 1) * HEAD_DIM] for h in range(heads_here)], axis=0
    )
    scores = _dot(queries, keys, ((1,), (1,))) * (1.0 / math.sqrt(HEAD_DIM))
    visible = kpos_ref[0, 0] <= qpos_ref[0]
    visible = jnp.concatenate([visible] * heads_here, axis=0)
    scores = jnp.where(visible, scores, -jnp.inf)
    row_max = jnp.max(scores, axis=1, keepdims=True)
    expo = jnp.exp(scores - row_max)
    probs = (expo / jnp.sum(expo, axis=1, keepdims=True)).astype(jnp.bfloat16)
    mixed = _dot(probs, values, ((1,), (0,))).astype(out_ref.dtype)
    rows = q_ref.shape[1]
    for h in range(heads_here):
        out_ref[0, :, h * HEAD_DIM:(h + 1) * HEAD_DIM] = mixed[h * rows:(h + 1) * rows]


def sparse_attend(sparse_query, store, store_index, key_pos, query_pos):
    seq_count, tok_count, lane_width = sparse_query.shape
    qblocks = tok_count // BLK
    kv_width = store.shape[-1]

    def listed(j):
        return pl.BlockSpec(
            (1, 2, BLK, kv_width), lambda s, b, idx: (idx[s, b * SEL + j], 0, 0, 0)
        )

    grid_spec = pltpu.PrefetchScalarGridSpec(
        num_scalar_prefetch=1,
        grid=(seq_count, qblocks),
        in_specs=[pl.BlockSpec((1, BLK, lane_width), lambda s, b, idx: (s, b, 0))]
        + [listed(j) for j in range(SEL)]
        + [
            pl.BlockSpec((1, 1, 1, SEL * BLK), lambda s, b, idx: (s, b, 0, 0)),
            pl.BlockSpec((1, BLK, 1), lambda s, b, idx: (b, 0, 0)),
        ],
        out_specs=pl.BlockSpec((1, BLK, lane_width), lambda s, b, idx: (s, b, 0)),
    )
    heads_here = lane_width // HEAD_DIM
    return pl.pallas_call(
        sparse_kernel,
        grid_spec=grid_spec,
        out_shape=jax.ShapeDtypeStruct(sparse_query.shape, sparse_query.dtype),
        compiler_params=pltpu.CompilerParams(dimension_semantics=("parallel", "parallel")),
        cost_estimate=pl.CostEstimate(
            flops=4 * seq_count * qblocks * heads_here * BLK * SEL * BLK * HEAD_DIM,
            transcendentals=seq_count * qblocks * heads_here * BLK * SEL * BLK,
            bytes_accessed=2 * 2 * seq_count * tok_count * lane_width + 4 * seq_count * qblocks * SEL * BLK * kv_width,
        ),
    )(store_index, sparse_query, *([store] * SEL), key_pos, query_pos)


def body(
    lin_query, lin_key, lin_value, lin_gain, sparse_query, sparse_key, sparse_value, block_lists
):
    seq_count, tok_count, lane_width = lin_query.shape
    heads_here = lane_width // HEAD_DIM
    ctx_pos = lax.axis_index("z") * lax.axis_size("y") + lax.axis_index("y")
    queries = lin_query.reshape(seq_count, tok_count, heads_here, HEAD_DIM)
    key_rows = lin_key.reshape(seq_count, tok_count, heads_here, HEAD_DIM)
    value_rows = lin_value.reshape(seq_count, tok_count, heads_here, HEAD_DIM)
    states = jnp.einsum("sjhd,sjhe->shde", key_rows, value_rows, preferred_element_type=jnp.float32)
    kv_width = sparse_key.shape[2]
    qblocks = tok_count // BLK
    ctx_count = lax.axis_size("z") * lax.axis_size("y")
    inside = linear_inside(lin_query, lin_key, lin_value)
    earlier, (inside, block_lists) = earlier_states(states, (inside, block_lists))
    store, store_index = listed_blocks(sparse_key, sparse_value, block_lists, ctx_pos, ctx_count)
    offsets = jnp.arange(BLK, dtype=jnp.int32)
    query_pos = ((ctx_pos * qblocks + jnp.arange(qblocks, dtype=jnp.int32)) * BLK)[:, None] + offsets[None, :]
    key_pos = (block_lists[:, :, :, None] * BLK + offsets).reshape(seq_count, qblocks, 1, SEL * BLK)
    sparse_out = sparse_attend(sparse_query, store, store_index, key_pos, query_pos[:, :, None])
    combined, row_squares = linear_finish(inside, lin_query, earlier)
    local_squares = row_squares[:, :, 0]
    whole_squares = lax.psum(local_squares, "head")
    inv_rms = lax.rsqrt(whole_squares / (HEADS * HEAD_DIM) + norm_eps)
    lin_out = (combined * inv_rms[:, :, None] * lin_gain).astype(jnp.bfloat16)
    return (lin_out, sparse_out)


def solution(mesh):
    in_specs = (
        P(None, "ctx", "head"),
        P(None, "ctx", "head"),
        P(None, "ctx", "head"),
        P("head"),
        P(None, "ctx", "head"),
        P(None, "ctx", "head"),
        P(None, "ctx", "head"),
        P(None, "ctx", None),
    )
    out_specs = (P(None, "ctx", "head"), P(None, "ctx", "head"))
    n_ctx, n_head = mesh.devices.shape
    y_count = 4 if n_ctx % 4 == 0 else 1
    grid = Mesh(mesh.devices.reshape(n_ctx // y_count, y_count, n_head), ("z", "y", "head"))

    def split(spec):
        return P(*[("z", "y") if part == "ctx" else part for part in spec])

    return jax.shard_map(
        body,
        mesh=grid,
        in_specs=tuple(split(s) for s in in_specs),
        out_specs=tuple(split(s) for s in out_specs),
        check_vma=False,
    )
```

```python
import math

import jax
import jax.numpy as jnp
from jax import lax
from jax.experimental import pallas as pl
from jax.experimental.pallas import tpu as pltpu
from jax.sharding import Mesh, PartitionSpec as P

HEADS = 64
HEAD_DIM = 128
BLK = 64
SEL = 8
CAP = 2


norm_eps = 1e-05


def earlier_states(states, cover_first, cover_second):
    y_pos = lax.axis_index("y")
    y_count = lax.axis_size("y")
    z_count = lax.axis_size("z")
    seq_count, heads_here, rows, cols = states.shape
    part_rows = rows // y_count
    quarters = states.reshape(seq_count, heads_here, y_count, part_rows, cols)

    def quarter(array, index):
        return lax.dynamic_index_in_dim(array, index, axis=2, keepdims=False)

    def cyclic(x, shift):
        return lax.ppermute(x, "y", [(i, (i + shift) % y_count) for i in range(y_count)])

    held = [quarter(quarters, y_pos)]
    for shift in range(1, y_count):
        held.append(cyclic(quarter(quarters, (y_pos + shift) % y_count), shift))
    held, cover_first = lax.optimization_barrier((held, cover_first()))
    sources = [(y_pos - shift) % y_count for shift in range(y_count)]
    group_total = sum(held[1:], held[0])
    below = []
    for shift in range(1, z_count):
        pairs = [(i, i + shift) for i in range(z_count - shift)]
        below.append(lax.ppermute(group_total, "z", pairs))
    below, covered = lax.optimization_barrier((below, cover_second(cover_first)))
    from_below = sum(below[1:], below[0])
    finished = []
    for target in range(y_count):
        within = from_below
        for source, piece in zip(sources, held):
            within = within + jnp.where(source < target, piece, 0.0)
        finished.append(within.astype(jnp.bfloat16))
    stacked = jnp.stack(finished)
    returned = [lax.dynamic_index_in_dim(stacked, y_pos, axis=0, keepdims=False)]
    for shift in range(1, y_count):
        outgoing = lax.dynamic_index_in_dim(stacked, (y_pos + shift) % y_count, axis=0, keepdims=False)
        returned.append(cyclic(outgoing, shift))
    by_shift = jnp.stack(returned)
    order = (y_pos - jnp.arange(y_count)) % y_count
    by_quarter = jnp.take(by_shift, order, axis=0)
    return jnp.moveaxis(by_quarter, 0, 2).reshape(seq_count, heads_here, rows, cols), covered


def listed_blocks(sparse_key, sparse_value, block_lists, ctx_pos, ctx_count):
    seq_count, tok_count, kv_width = sparse_key.shape
    qblocks = tok_count // BLK
    kv_blocks = jnp.stack(
        [sparse_key.reshape(seq_count, qblocks, BLK, kv_width),
         sparse_value.reshape(seq_count, qblocks, BLK, kv_width)],
        axis=2,
    )
    own_lists = block_lists.reshape(seq_count, qblocks * SEL)
    listed_here = jnp.any(
        own_lists[:, :, None] == jnp.arange(ctx_count * qblocks, dtype=jnp.int32), axis=1
    ).reshape(seq_count, ctx_count, qblocks)
    rank = jnp.cumsum(listed_here.astype(jnp.int32), axis=-1)
    wanted = jnp.stack(
        [jnp.argmax(listed_here & (rank == slot + 1), axis=-1) for slot in range(CAP)], axis=-1
    ).astype(jnp.int32)
    requests = jnp.moveaxis(wanted, 1, 0)
    asked = lax.all_to_all(requests, ("z", "y"), 0, 0, tiled=True)
    send_index = (asked + jnp.arange(seq_count, dtype=jnp.int32)[None, :, None] * qblocks).reshape(-1)
    outgoing = jnp.take(kv_blocks.reshape(seq_count * qblocks, 2, BLK, kv_width), send_index, axis=0)
    arrived = lax.all_to_all(outgoing, ("z", "y"), 0, 0, tiled=True)
    store = jnp.concatenate(
        [kv_blocks.reshape(seq_count * qblocks, 2, BLK, kv_width), arrived], axis=0
    )
    own_rank = (rank - 1).reshape(seq_count, ctx_count * qblocks)
    slot = jnp.take_along_axis(own_rank, own_lists, axis=1)
    source = own_lists // qblocks
    local = own_lists % qblocks
    seq_ids = jnp.arange(seq_count, dtype=jnp.int32)[:, None]
    remote = seq_count * qblocks + (source * seq_count + seq_ids) * CAP + slot
    store_index = jnp.where(source == ctx_pos, seq_ids * qblocks + local, remote)
    store_index = jnp.clip(store_index, 0, store.shape[0] - 1)
    return store, store_index.astype(jnp.int32)


def _dot(a, b, contract):
    return lax.dot_general(a, b, (contract, ((), ())), preferred_element_type=jnp.float32)


def inside_kernel(q_ref, k_ref, v_ref, out_ref):
    scores = _dot(q_ref[0], k_ref[0], ((1,), (1,)))
    rows = lax.broadcasted_iota(jnp.int32, scores.shape, 0)
    cols = lax.broadcasted_iota(jnp.int32, scores.shape, 1)
    weights = jnp.where(rows >= cols, scores, 0.0).astype(jnp.bfloat16)
    out_ref[0] = _dot(weights, v_ref[0], ((1,), (0,)))


def finish_kernel(inside_ref, q_ref, e_ref, out_ref, sq_ref):
    heads_here = e_ref.shape[1]
    total = None
    for h in range(heads_here):
        lanes = slice(h * HEAD_DIM, (h + 1) * HEAD_DIM)
        combined = inside_ref[0, :, lanes] + _dot(q_ref[0, :, lanes], e_ref[0, h], ((1,), (0,)))
        out_ref[0, :, lanes] = combined
        squares = jnp.sum(combined * combined, axis=1, keepdims=True)
        total = squares if total is None else total + squares
    sq_ref[0] = total


def linear_inside(lin_query, lin_key, lin_value):
    seq_count, tok_count, lane_width = lin_query.shape
    heads_here = lane_width // HEAD_DIM
    tile = pl.BlockSpec((1, tok_count, HEAD_DIM), lambda s, h: (s, 0, h))
    return pl.pallas_call(
        inside_kernel,
        grid=(seq_count, heads_here),
        in_specs=[tile, tile, tile],
        out_specs=tile,
        out_shape=jax.ShapeDtypeStruct((seq_count, tok_count, lane_width), jnp.float32),
        compiler_params=pltpu.CompilerParams(dimension_semantics=("parallel", "parallel")),
        cost_estimate=pl.CostEstimate(
            flops=4 * seq_count * heads_here * tok_count * tok_count * HEAD_DIM,
            transcendentals=0,
            bytes_accessed=seq_count * tok_count * lane_width * (3 * 2 + 4),
        ),
    )(lin_query, lin_key, lin_value)


def linear_finish(inside, lin_query, earlier):
    seq_count, tok_count, lane_width = lin_query.shape
    heads_here = lane_width // HEAD_DIM
    rows = pl.BlockSpec((1, tok_count, lane_width), lambda s: (s, 0, 0))
    return pl.pallas_call(
        finish_kernel,
        grid=(seq_count,),
        in_specs=[rows, rows, pl.BlockSpec((1, heads_here, HEAD_DIM, HEAD_DIM), lambda s: (s, 0, 0, 0))],
        out_specs=[rows, pl.BlockSpec((1, tok_count, 1), lambda s: (s, 0, 0))],
        out_shape=[
            jax.ShapeDtypeStruct((seq_count, tok_count, lane_width), jnp.float32),
            jax.ShapeDtypeStruct((seq_count, tok_count, 1), jnp.float32),
        ],
        compiler_params=pltpu.CompilerParams(dimension_semantics=("parallel",)),
        cost_estimate=pl.CostEstimate(
            flops=2 * seq_count * heads_here * tok_count * HEAD_DIM * HEAD_DIM,
            transcendentals=0,
            bytes_accessed=seq_count * tok_count * lane_width * (2 + 4 + 4),
        ),
    )(inside, lin_query, earlier)


def sparse_kernel(index_ref, q_ref, *refs):
    block_refs = refs[:SEL]
    kpos_ref, qpos_ref, out_ref = refs[SEL], refs[SEL + 1], refs[-1]
    keys = jnp.concatenate([r[0, 0] for r in block_refs], axis=0)
    values = jnp.concatenate([r[0, 1] for r in block_refs], axis=0)
    heads_here = q_ref.shape[2] // HEAD_DIM
    queries = jnp.concatenate(
        [q_ref[0, :, h * HEAD_DIM:(h + 1) * HEAD_DIM] for h in range(heads_here)], axis=0
    )
    scores = _dot(queries, keys, ((1,), (1,))) * (1.0 / math.sqrt(HEAD_DIM))
    visible = kpos_ref[0, 0] <= qpos_ref[0]
    visible = jnp.concatenate([visible] * heads_here, axis=0)
    scores = jnp.where(visible, scores, -jnp.inf)
    row_max = jnp.max(scores, axis=1, keepdims=True)
    expo = jnp.exp(scores - row_max)
    probs = (expo / jnp.sum(expo, axis=1, keepdims=True)).astype(jnp.bfloat16)
    mixed = _dot(probs, values, ((1,), (0,))).astype(out_ref.dtype)
    rows = q_ref.shape[1]
    for h in range(heads_here):
        out_ref[0, :, h * HEAD_DIM:(h + 1) * HEAD_DIM] = mixed[h * rows:(h + 1) * rows]


def sparse_attend(sparse_query, store, store_index, key_pos, query_pos, first, count, prior=None):
    seq_count, tok_count, lane_width = sparse_query.shape
    qblocks = tok_count // BLK
    kv_width = store.shape[-1]

    def listed(j):
        return pl.BlockSpec(
            (1, 2, BLK, kv_width), lambda s, b, idx: (idx[s + first, b * SEL + j], 0, 0, 0)
        )

    in_specs = (
        [pl.BlockSpec((1, BLK, lane_width), lambda s, b, idx: (s + first, b, 0))]
        + [listed(j) for j in range(SEL)]
        + [
            pl.BlockSpec((1, 1, 1, SEL * BLK), lambda s, b, idx: (s + first, b, 0, 0)),
            pl.BlockSpec((1, BLK, 1), lambda s, b, idx: (b, 0, 0)),
        ]
    )
    operands = [sparse_query] + [store] * SEL + [key_pos, query_pos]
    aliases = {}
    if prior is not None:
        in_specs.append(pl.BlockSpec(memory_space=pl.ANY))
        aliases = {1 + len(operands): 0}
        operands.append(prior)
    grid_spec = pltpu.PrefetchScalarGridSpec(
        num_scalar_prefetch=1,
        grid=(count, qblocks),
        in_specs=in_specs,
        out_specs=pl.BlockSpec((1, BLK, lane_width), lambda s, b, idx: (s + first, b, 0)),
    )
    heads_here = lane_width // HEAD_DIM
    return pl.pallas_call(
        sparse_kernel,
        grid_spec=grid_spec,
        out_shape=jax.ShapeDtypeStruct(sparse_query.shape, sparse_query.dtype),
        input_output_aliases=aliases,
        compiler_params=pltpu.CompilerParams(dimension_semantics=("parallel", "parallel")),
        cost_estimate=pl.CostEstimate(
            flops=4 * count * qblocks * heads_here * BLK * SEL * BLK * HEAD_DIM,
            transcendentals=count * qblocks * heads_here * BLK * SEL * BLK,
            bytes_accessed=2 * 2 * count * tok_count * lane_width + 4 * count * qblocks * SEL * BLK * kv_width,
        ),
    )(store_index, *operands)


def body(
    lin_query, lin_key, lin_value, lin_gain, sparse_query, sparse_key, sparse_value, block_lists
):
    seq_count, tok_count, lane_width = lin_query.shape
    heads_here = lane_width // HEAD_DIM
    ctx_pos = lax.axis_index("z") * lax.axis_size("y") + lax.axis_index("y")
    queries = lin_query.reshape(seq_count, tok_count, heads_here, HEAD_DIM)
    key_rows = lin_key.reshape(seq_count, tok_count, heads_here, HEAD_DIM)
    value_rows = lin_value.reshape(seq_count, tok_count, heads_here, HEAD_DIM)
    states = jnp.einsum("sjhd,sjhe->shde", key_rows, value_rows, preferred_element_type=jnp.float32)
    kv_width = sparse_key.shape[2]
    qblocks = tok_count // BLK
    ctx_count = lax.axis_size("z") * lax.axis_size("y")
    store, store_index = listed_blocks(sparse_key, sparse_value, block_lists, ctx_pos, ctx_count)
    inside = linear_inside(lin_query, lin_key, lin_value)
    states, store, inside = lax.optimization_barrier((states, store, inside))
    offsets = jnp.arange(BLK, dtype=jnp.int32)
    query_pos = ((ctx_pos * qblocks + jnp.arange(qblocks, dtype=jnp.int32)) * BLK)[:, None] + offsets[None, :]
    key_pos = (block_lists[:, :, :, None] * BLK + offsets).reshape(seq_count, qblocks, 1, SEL * BLK)
    query_pos = query_pos[:, :, None]

    def first_part():
        return sparse_attend(sparse_query, store, store_index, key_pos, query_pos, 0, 1)

    def second_part(prior):
        return sparse_attend(sparse_query, store, store_index, key_pos, query_pos, 1, seq_count - 1, prior)

    earlier, sparse_out = earlier_states(states, first_part, second_part)
    combined, row_squares = linear_finish(inside, lin_query, earlier)
    local_squares = row_squares[:, :, 0]
    whole_squares = lax.psum(local_squares, "head")
    inv_rms = lax.rsqrt(whole_squares / (HEADS * HEAD_DIM) + norm_eps)
    lin_out = (combined * inv_rms[:, :, None] * lin_gain).astype(jnp.bfloat16)
    return (lin_out, sparse_out)


def solution(mesh):
    in_specs = (
        P(None, "ctx", "head"),
        P(None, "ctx", "head"),
        P(None, "ctx", "head"),
        P("head"),
        P(None, "ctx", "head"),
        P(None, "ctx", "head"),
        P(None, "ctx", "head"),
        P(None, "ctx", None),
    )
    out_specs = (P(None, "ctx", "head"), P(None, "ctx", "head"))
    n_ctx, n_head = mesh.devices.shape
    y_count = 4 if n_ctx % 4 == 0 else 1
    grid = Mesh(mesh.devices.reshape(n_ctx // y_count, y_count, n_head), ("z", "y", "head"))

    def split(spec):
        return P(*[("z", "y") if part == "ctx" else part for part in spec])

    return jax.shard_map(
        body,
        mesh=grid,
        in_specs=tuple(split(s) for s in in_specs),
        out_specs=tuple(split(s) for s in out_specs),
        check_vma=False,
    )
```

```python
import math

import jax
import jax.numpy as jnp
from jax import lax
from jax.experimental import pallas as pl
from jax.experimental.pallas import tpu as pltpu
from jax.sharding import Mesh, PartitionSpec as P

HEADS = 64
HEAD_DIM = 128
BLK = 64
SEL = 8
CAP = 2


norm_eps = 1e-05


def earlier_states(states, cover_first, cover_second, cover_third):
    y_pos = lax.axis_index("y")
    y_count = lax.axis_size("y")
    z_count = lax.axis_size("z")
    seq_count, heads_here, rows, cols = states.shape
    part_rows = rows // y_count
    quarters = states.reshape(seq_count, heads_here, y_count, part_rows, cols)

    def quarter(array, index):
        return lax.dynamic_index_in_dim(array, index, axis=2, keepdims=False)

    def cyclic(x, shift):
        return lax.ppermute(x, "y", [(i, (i + shift) % y_count) for i in range(y_count)])

    held = [quarter(quarters, y_pos)]
    for shift in range(1, y_count):
        held.append(cyclic(quarter(quarters, (y_pos + shift) % y_count), shift))
    held, cover_first = lax.optimization_barrier((held, cover_first()))
    sources = [(y_pos - shift) % y_count for shift in range(y_count)]
    group_total = sum(held[1:], held[0])
    below = []
    for shift in range(1, z_count):
        pairs = [(i, i + shift) for i in range(z_count - shift)]
        below.append(lax.ppermute(group_total, "z", pairs))
    below, covered = lax.optimization_barrier((below, cover_second(cover_first)))
    from_below = sum(below[1:], below[0])
    finished = []
    for target in range(y_count):
        within = from_below
        for source, piece in zip(sources, held):
            within = within + jnp.where(source < target, piece, 0.0)
        finished.append(within.astype(jnp.bfloat16))
    stacked = jnp.stack(finished)
    returned = [lax.dynamic_index_in_dim(stacked, y_pos, axis=0, keepdims=False)]
    for shift in range(1, y_count):
        outgoing = lax.dynamic_index_in_dim(stacked, (y_pos + shift) % y_count, axis=0, keepdims=False)
        returned.append(cyclic(outgoing, shift))
    returned, covered = lax.optimization_barrier((returned, cover_third(covered)))
    by_shift = jnp.stack(returned)
    order = (y_pos - jnp.arange(y_count)) % y_count
    by_quarter = jnp.take(by_shift, order, axis=0)
    return jnp.moveaxis(by_quarter, 0, 2).reshape(seq_count, heads_here, rows, cols), covered


def listed_blocks(sparse_key, sparse_value, block_lists, ctx_pos, ctx_count):
    seq_count, tok_count, kv_width = sparse_key.shape
    qblocks = tok_count // BLK
    kv_blocks = jnp.stack(
        [sparse_key.reshape(seq_count, qblocks, BLK, kv_width),
         sparse_value.reshape(seq_count, qblocks, BLK, kv_width)],
        axis=2,
    )
    own_lists = block_lists.reshape(seq_count, qblocks * SEL)
    listed_here = jnp.any(
        own_lists[:, :, None] == jnp.arange(ctx_count * qblocks, dtype=jnp.int32), axis=1
    ).reshape(seq_count, ctx_count, qblocks)
    rank = jnp.cumsum(listed_here.astype(jnp.int32), axis=-1)
    wanted = jnp.stack(
        [jnp.argmax(listed_here & (rank == slot + 1), axis=-1) for slot in range(CAP)], axis=-1
    ).astype(jnp.int32)
    requests = jnp.moveaxis(wanted, 1, 0)
    asked = lax.all_to_all(requests, ("z", "y"), 0, 0, tiled=True)
    send_index = (asked + jnp.arange(seq_count, dtype=jnp.int32)[None, :, None] * qblocks).reshape(-1)
    outgoing = jnp.take(kv_blocks.reshape(seq_count * qblocks, 2, BLK, kv_width), send_index, axis=0)
    arrived = lax.all_to_all(outgoing, ("z", "y"), 0, 0, tiled=True)
    store = jnp.concatenate(
        [kv_blocks.reshape(seq_count * qblocks, 2, BLK, kv_width), arrived], axis=0
    )
    own_rank = (rank - 1).reshape(seq_count, ctx_count * qblocks)
    slot = jnp.take_along_axis(own_rank, own_lists, axis=1)
    source = own_lists // qblocks
    local = own_lists % qblocks
    seq_ids = jnp.arange(seq_count, dtype=jnp.int32)[:, None]
    remote = seq_count * qblocks + (source * seq_count + seq_ids) * CAP + slot
    store_index = jnp.where(source == ctx_pos, seq_ids * qblocks + local, remote)
    store_index = jnp.clip(store_index, 0, store.shape[0] - 1)
    return store, store_index.astype(jnp.int32)


def _dot(a, b, contract):
    return lax.dot_general(a, b, (contract, ((), ())), preferred_element_type=jnp.float32)


def inside_kernel(q_ref, k_ref, v_ref, out_ref):
    scores = _dot(q_ref[0], k_ref[0], ((1,), (1,)))
    rows = lax.broadcasted_iota(jnp.int32, scores.shape, 0)
    cols = lax.broadcasted_iota(jnp.int32, scores.shape, 1)
    weights = jnp.where(rows >= cols, scores, 0.0).astype(jnp.bfloat16)
    out_ref[0] = _dot(weights, v_ref[0], ((1,), (0,)))


def finish_kernel(inside_ref, q_ref, e_ref, out_ref, sq_ref):
    heads_here = e_ref.shape[1]
    total = None
    for h in range(heads_here):
        lanes = slice(h * HEAD_DIM, (h + 1) * HEAD_DIM)
        combined = inside_ref[0, :, lanes] + _dot(q_ref[0, :, lanes], e_ref[0, h], ((1,), (0,)))
        out_ref[0, :, lanes] = combined
        squares = jnp.sum(combined * combined, axis=1, keepdims=True)
        total = squares if total is None else total + squares
    sq_ref[0] = total


def linear_inside(lin_query, lin_key, lin_value):
    seq_count, tok_count, lane_width = lin_query.shape
    heads_here = lane_width // HEAD_DIM
    tile = pl.BlockSpec((1, tok_count, HEAD_DIM), lambda s, h: (s, 0, h))
    return pl.pallas_call(
        inside_kernel,
        grid=(seq_count, heads_here),
        in_specs=[tile, tile, tile],
        out_specs=tile,
        out_shape=jax.ShapeDtypeStruct((seq_count, tok_count, lane_width), jnp.float32),
        compiler_params=pltpu.CompilerParams(dimension_semantics=("parallel", "parallel")),
        cost_estimate=pl.CostEstimate(
            flops=4 * seq_count * heads_here * tok_count * tok_count * HEAD_DIM,
            transcendentals=0,
            bytes_accessed=seq_count * tok_count * lane_width * (3 * 2 + 4),
        ),
    )(lin_query, lin_key, lin_value)


def linear_finish(inside, lin_query, earlier):
    seq_count, tok_count, lane_width = lin_query.shape
    heads_here = lane_width // HEAD_DIM
    rows = pl.BlockSpec((1, tok_count, lane_width), lambda s: (s, 0, 0))
    return pl.pallas_call(
        finish_kernel,
        grid=(seq_count,),
        in_specs=[rows, rows, pl.BlockSpec((1, heads_here, HEAD_DIM, HEAD_DIM), lambda s: (s, 0, 0, 0))],
        out_specs=[rows, pl.BlockSpec((1, tok_count, 1), lambda s: (s, 0, 0))],
        out_shape=[
            jax.ShapeDtypeStruct((seq_count, tok_count, lane_width), jnp.float32),
            jax.ShapeDtypeStruct((seq_count, tok_count, 1), jnp.float32),
        ],
        compiler_params=pltpu.CompilerParams(dimension_semantics=("parallel",)),
        cost_estimate=pl.CostEstimate(
            flops=2 * seq_count * heads_here * tok_count * HEAD_DIM * HEAD_DIM,
            transcendentals=0,
            bytes_accessed=seq_count * tok_count * lane_width * (2 + 4 + 4),
        ),
    )(inside, lin_query, earlier)


def sparse_kernel(index_ref, q_ref, *refs):
    block_refs = refs[:SEL]
    kpos_ref, qpos_ref, out_ref = refs[SEL], refs[SEL + 1], refs[-1]
    keys = jnp.concatenate([r[0, 0] for r in block_refs], axis=0)
    values = jnp.concatenate([r[0, 1] for r in block_refs], axis=0)
    heads_here = q_ref.shape[2] // HEAD_DIM
    queries = jnp.concatenate(
        [q_ref[0, :, h * HEAD_DIM:(h + 1) * HEAD_DIM] for h in range(heads_here)], axis=0
    )
    scores = _dot(queries, keys, ((1,), (1,))) * (1.0 / math.sqrt(HEAD_DIM))
    visible = kpos_ref[0, 0] <= qpos_ref[0]
    visible = jnp.concatenate([visible] * heads_here, axis=0)
    scores = jnp.where(visible, scores, -jnp.inf)
    row_max = jnp.max(scores, axis=1, keepdims=True)
    expo = jnp.exp(scores - row_max)
    probs = (expo / jnp.sum(expo, axis=1, keepdims=True)).astype(jnp.bfloat16)
    mixed = _dot(probs, values, ((1,), (0,))).astype(out_ref.dtype)
    rows = q_ref.shape[1]
    for h in range(heads_here):
        out_ref[0, :, h * HEAD_DIM:(h + 1) * HEAD_DIM] = mixed[h * rows:(h + 1) * rows]


def sparse_attend(sparse_query, store, store_index, key_pos, query_pos, first, count, prior=None):
    seq_count, tok_count, lane_width = sparse_query.shape
    qblocks = tok_count // BLK
    kv_width = store.shape[-1]

    def listed(j):
        return pl.BlockSpec(
            (1, 2, BLK, kv_width), lambda s, b, idx: (idx[s + first, b * SEL + j], 0, 0, 0)
        )

    in_specs = (
        [pl.BlockSpec((1, BLK, lane_width), lambda s, b, idx: (s + first, b, 0))]
        + [listed(j) for j in range(SEL)]
        + [
            pl.BlockSpec((1, 1, 1, SEL * BLK), lambda s, b, idx: (s + first, b, 0, 0)),
            pl.BlockSpec((1, BLK, 1), lambda s, b, idx: (b, 0, 0)),
        ]
    )
    operands = [sparse_query] + [store] * SEL + [key_pos, query_pos]
    aliases = {}
    if prior is not None:
        in_specs.append(pl.BlockSpec(memory_space=pl.ANY))
        aliases = {1 + len(operands): 0}
        operands.append(prior)
    grid_spec = pltpu.PrefetchScalarGridSpec(
        num_scalar_prefetch=1,
        grid=(count, qblocks),
        in_specs=in_specs,
        out_specs=pl.BlockSpec((1, BLK, lane_width), lambda s, b, idx: (s + first, b, 0)),
    )
    heads_here = lane_width // HEAD_DIM
    return pl.pallas_call(
        sparse_kernel,
        grid_spec=grid_spec,
        out_shape=jax.ShapeDtypeStruct(sparse_query.shape, sparse_query.dtype),
        input_output_aliases=aliases,
        compiler_params=pltpu.CompilerParams(dimension_semantics=("parallel", "parallel")),
        cost_estimate=pl.CostEstimate(
            flops=4 * count * qblocks * heads_here * BLK * SEL * BLK * HEAD_DIM,
            transcendentals=count * qblocks * heads_here * BLK * SEL * BLK,
            bytes_accessed=2 * 2 * count * tok_count * lane_width + 4 * count * qblocks * SEL * BLK * kv_width,
        ),
    )(store_index, *operands)


def body(
    lin_query, lin_key, lin_value, lin_gain, sparse_query, sparse_key, sparse_value, block_lists
):
    seq_count, tok_count, lane_width = lin_query.shape
    heads_here = lane_width // HEAD_DIM
    ctx_pos = lax.axis_index("z") * lax.axis_size("y") + lax.axis_index("y")
    queries = lin_query.reshape(seq_count, tok_count, heads_here, HEAD_DIM)
    key_rows = lin_key.reshape(seq_count, tok_count, heads_here, HEAD_DIM)
    value_rows = lin_value.reshape(seq_count, tok_count, heads_here, HEAD_DIM)
    states = jnp.einsum("sjhd,sjhe->shde", key_rows, value_rows, preferred_element_type=jnp.float32)
    kv_width = sparse_key.shape[2]
    qblocks = tok_count // BLK
    ctx_count = lax.axis_size("z") * lax.axis_size("y")
    store, store_index = listed_blocks(sparse_key, sparse_value, block_lists, ctx_pos, ctx_count)
    inside = linear_inside(lin_query, lin_key, lin_value)
    states, store, inside = lax.optimization_barrier((states, store, inside))
    offsets = jnp.arange(BLK, dtype=jnp.int32)
    query_pos = ((ctx_pos * qblocks + jnp.arange(qblocks, dtype=jnp.int32)) * BLK)[:, None] + offsets[None, :]
    key_pos = (block_lists[:, :, :, None] * BLK + offsets).reshape(seq_count, qblocks, 1, SEL * BLK)
    query_pos = query_pos[:, :, None]

    def first_part():
        return sparse_attend(sparse_query, store, store_index, key_pos, query_pos, 0, 1)

    def second_part(prior):
        return sparse_attend(sparse_query, store, store_index, key_pos, query_pos, 1, 1, prior)

    def third_part(prior):
        return sparse_attend(sparse_query, store, store_index, key_pos, query_pos, 2, seq_count - 2, prior)

    earlier, sparse_out = earlier_states(states, first_part, second_part, third_part)
    combined, row_squares = linear_finish(inside, lin_query, earlier)
    local_squares = row_squares[:, :, 0]
    whole_squares = lax.psum(local_squares, "head")
    inv_rms = lax.rsqrt(whole_squares / (HEADS * HEAD_DIM) + norm_eps)
    lin_out = (combined * inv_rms[:, :, None] * lin_gain).astype(jnp.bfloat16)
    return (lin_out, sparse_out)


def solution(mesh):
    in_specs = (
        P(None, "ctx", "head"),
        P(None, "ctx", "head"),
        P(None, "ctx", "head"),
        P("head"),
        P(None, "ctx", "head"),
        P(None, "ctx", "head"),
        P(None, "ctx", "head"),
        P(None, "ctx", None),
    )
    out_specs = (P(None, "ctx", "head"), P(None, "ctx", "head"))
    n_ctx, n_head = mesh.devices.shape
    y_count = 4 if n_ctx % 4 == 0 else 1
    grid = Mesh(mesh.devices.reshape(n_ctx // y_count, y_count, n_head), ("z", "y", "head"))

    def split(spec):
        return P(*[("z", "y") if part == "ctx" else part for part in spec])

    return jax.shard_map(
        body,
        mesh=grid,
        in_specs=tuple(split(s) for s in in_specs),
        out_specs=tuple(split(s) for s in out_specs),
        check_vma=False,
    )
```

```python
import math

import jax
import jax.numpy as jnp
from jax import lax
from jax.experimental import pallas as pl
from jax.experimental.pallas import tpu as pltpu
from jax.sharding import Mesh, PartitionSpec as P

HEADS = 64
HEAD_DIM = 128
BLK = 64
SEL = 8
CAP = 2


norm_eps = 1e-05


def earlier_states(states, cover_first, cover_second, cover_third):
    y_pos = lax.axis_index("y")
    y_count = lax.axis_size("y")
    z_count = lax.axis_size("z")
    seq_count, heads_here, rows, cols = states.shape
    part_rows = rows // y_count
    quarters = states.reshape(seq_count, heads_here, y_count, part_rows, cols)

    def quarter(array, index):
        return lax.dynamic_index_in_dim(array, index, axis=2, keepdims=False)

    def cyclic(x, shift):
        return lax.ppermute(x, "y", [(i, (i + shift) % y_count) for i in range(y_count)])

    held = [quarter(quarters, y_pos)]
    for shift in range(1, y_count):
        held.append(cyclic(quarter(quarters, (y_pos + shift) % y_count), shift))
    held, cover_first = lax.optimization_barrier((held, cover_first()))
    sources = [(y_pos - shift) % y_count for shift in range(y_count)]
    group_total = sum(held[1:], held[0])
    below = []
    for shift in range(1, z_count):
        pairs = [(i, i + shift) for i in range(z_count - shift)]
        below.append(lax.ppermute(group_total, "z", pairs))
    below, covered = lax.optimization_barrier((below, cover_second(cover_first)))
    from_below = sum(below[1:], below[0])
    finished = []
    for target in range(y_count):
        within = from_below
        for source, piece in zip(sources, held):
            within = within + jnp.where(source < target, piece, 0.0)
        finished.append(within.astype(jnp.bfloat16))
    stacked = jnp.stack(finished)
    returned = [lax.dynamic_index_in_dim(stacked, y_pos, axis=0, keepdims=False)]
    for shift in range(1, y_count):
        outgoing = lax.dynamic_index_in_dim(stacked, (y_pos + shift) % y_count, axis=0, keepdims=False)
        returned.append(cyclic(outgoing, shift))
    returned, covered = lax.optimization_barrier((returned, cover_third(covered)))
    by_shift = jnp.stack(returned)
    order = (y_pos - jnp.arange(y_count)) % y_count
    by_quarter = jnp.take(by_shift, order, axis=0)
    return jnp.moveaxis(by_quarter, 0, 2).reshape(seq_count, heads_here, rows, cols), covered


def listed_blocks(sparse_key, sparse_value, block_lists, ctx_pos, ctx_count):
    seq_count, tok_count, kv_width = sparse_key.shape
    qblocks = tok_count // BLK
    kv_blocks = jnp.stack(
        [sparse_key.reshape(seq_count, qblocks, BLK, kv_width),
         sparse_value.reshape(seq_count, qblocks, BLK, kv_width)],
        axis=2,
    )
    own_lists = block_lists.reshape(seq_count, qblocks * SEL)
    listed_here = jnp.any(
        own_lists[:, :, None] == jnp.arange(ctx_count * qblocks, dtype=jnp.int32), axis=1
    ).reshape(seq_count, ctx_count, qblocks)
    rank = jnp.cumsum(listed_here.astype(jnp.int32), axis=-1)
    wanted = jnp.stack(
        [jnp.argmax(listed_here & (rank == slot + 1), axis=-1) for slot in range(CAP)], axis=-1
    ).astype(jnp.int32)
    requests = jnp.moveaxis(wanted, 1, 0)
    asked = lax.all_to_all(requests, ("z", "y"), 0, 0, tiled=True)
    send_index = (asked + jnp.arange(seq_count, dtype=jnp.int32)[None, :, None] * qblocks).reshape(-1)
    outgoing = jnp.take(kv_blocks.reshape(seq_count * qblocks, 2, BLK, kv_width), send_index, axis=0)
    arrived = lax.all_to_all(outgoing, ("z", "y"), 0, 0, tiled=True)
    store = jnp.concatenate(
        [kv_blocks.reshape(seq_count * qblocks, 2, BLK, kv_width), arrived], axis=0
    )
    own_rank = (rank - 1).reshape(seq_count, ctx_count * qblocks)
    slot = jnp.take_along_axis(own_rank, own_lists, axis=1)
    source = own_lists // qblocks
    local = own_lists % qblocks
    seq_ids = jnp.arange(seq_count, dtype=jnp.int32)[:, None]
    remote = seq_count * qblocks + (source * seq_count + seq_ids) * CAP + slot
    store_index = jnp.where(source == ctx_pos, seq_ids * qblocks + local, remote)
    store_index = jnp.clip(store_index, 0, store.shape[0] - 1)
    return store, store_index.astype(jnp.int32)


def _dot(a, b, contract):
    return lax.dot_general(a, b, (contract, ((), ())), preferred_element_type=jnp.float32)


def inside_kernel(q_ref, k_ref, v_ref, out_ref):
    scores = _dot(q_ref[0], k_ref[0], ((1,), (1,)))
    rows = lax.broadcasted_iota(jnp.int32, scores.shape, 0)
    cols = lax.broadcasted_iota(jnp.int32, scores.shape, 1)
    weights = jnp.where(rows >= cols, scores, 0.0).astype(jnp.bfloat16)
    out_ref[0] = _dot(weights, v_ref[0], ((1,), (0,)))


def finish_kernel(inside_ref, q_ref, e_ref, out_ref, sq_ref):
    heads_here = e_ref.shape[1]
    total = None
    for h in range(heads_here):
        lanes = slice(h * HEAD_DIM, (h + 1) * HEAD_DIM)
        combined = inside_ref[0, :, lanes] + _dot(q_ref[0, :, lanes], e_ref[0, h], ((1,), (0,)))
        out_ref[0, :, lanes] = combined
        squares = jnp.sum(combined * combined, axis=1, keepdims=True)
        total = squares if total is None else total + squares
    sq_ref[0] = total


def linear_inside(lin_query, lin_key, lin_value):
    seq_count, tok_count, lane_width = lin_query.shape
    heads_here = lane_width // HEAD_DIM
    tile = pl.BlockSpec((1, tok_count, HEAD_DIM), lambda s, h: (s, 0, h))
    return pl.pallas_call(
        inside_kernel,
        grid=(seq_count, heads_here),
        in_specs=[tile, tile, tile],
        out_specs=tile,
        out_shape=jax.ShapeDtypeStruct((seq_count, tok_count, lane_width), jnp.float32),
        compiler_params=pltpu.CompilerParams(dimension_semantics=("parallel", "parallel")),
        cost_estimate=pl.CostEstimate(
            flops=4 * seq_count * heads_here * tok_count * tok_count * HEAD_DIM,
            transcendentals=0,
            bytes_accessed=seq_count * tok_count * lane_width * (3 * 2 + 4),
        ),
    )(lin_query, lin_key, lin_value)


def linear_finish(inside, lin_query, earlier):
    seq_count, tok_count, lane_width = lin_query.shape
    heads_here = lane_width // HEAD_DIM
    rows = pl.BlockSpec((1, tok_count, lane_width), lambda s: (s, 0, 0))
    return pl.pallas_call(
        finish_kernel,
        grid=(seq_count,),
        in_specs=[rows, rows, pl.BlockSpec((1, heads_here, HEAD_DIM, HEAD_DIM), lambda s: (s, 0, 0, 0))],
        out_specs=[rows, pl.BlockSpec((1, tok_count, 1), lambda s: (s, 0, 0))],
        out_shape=[
            jax.ShapeDtypeStruct((seq_count, tok_count, lane_width), jnp.float32),
            jax.ShapeDtypeStruct((seq_count, tok_count, 1), jnp.float32),
        ],
        compiler_params=pltpu.CompilerParams(dimension_semantics=("parallel",)),
        cost_estimate=pl.CostEstimate(
            flops=2 * seq_count * heads_here * tok_count * HEAD_DIM * HEAD_DIM,
            transcendentals=0,
            bytes_accessed=seq_count * tok_count * lane_width * (2 + 4 + 4),
        ),
    )(inside, lin_query, earlier)


def sparse_kernel(index_ref, q_ref, *refs):
    block_refs = refs[:SEL]
    kpos_ref, qpos_ref, out_ref = refs[SEL], refs[SEL + 1], refs[-1]
    keys = jnp.concatenate([r[0, 0] for r in block_refs], axis=0)
    values = jnp.concatenate([r[0, 1] for r in block_refs], axis=0)
    heads_here = q_ref.shape[2] // HEAD_DIM
    queries = jnp.concatenate(
        [q_ref[0, :, h * HEAD_DIM:(h + 1) * HEAD_DIM] for h in range(heads_here)], axis=0
    )
    scores = _dot(queries, keys, ((1,), (1,))) * (1.0 / math.sqrt(HEAD_DIM))
    visible = kpos_ref[0, 0] <= qpos_ref[0]
    visible = jnp.concatenate([visible] * heads_here, axis=0)
    scores = jnp.where(visible, scores, -jnp.inf)
    row_max = jnp.max(scores, axis=1, keepdims=True)
    expo = jnp.exp(scores - row_max)
    probs = (expo / jnp.sum(expo, axis=1, keepdims=True)).astype(jnp.bfloat16)
    mixed = _dot(probs, values, ((1,), (0,))).astype(out_ref.dtype)
    rows = q_ref.shape[1]
    for h in range(heads_here):
        out_ref[0, :, h * HEAD_DIM:(h + 1) * HEAD_DIM] = mixed[h * rows:(h + 1) * rows]


def sparse_attend(sparse_query, store, store_index, key_pos, query_pos, first, count, prior=None):
    seq_count, tok_count, lane_width = sparse_query.shape
    qblocks = tok_count // BLK
    kv_width = store.shape[-1]

    def listed(j):
        return pl.BlockSpec(
            (1, 2, BLK, kv_width), lambda s, b, idx: (idx[s + first, b * SEL + j], 0, 0, 0)
        )

    in_specs = (
        [pl.BlockSpec((1, BLK, lane_width), lambda s, b, idx: (s + first, b, 0))]
        + [listed(j) for j in range(SEL)]
        + [
            pl.BlockSpec((1, 1, 1, SEL * BLK), lambda s, b, idx: (s + first, b, 0, 0)),
            pl.BlockSpec((1, BLK, 1), lambda s, b, idx: (b, 0, 0)),
        ]
    )
    operands = [sparse_query] + [store] * SEL + [key_pos, query_pos]
    aliases = {}
    if prior is not None:
        in_specs.append(pl.BlockSpec(memory_space=pl.ANY))
        aliases = {1 + len(operands): 0}
        operands.append(prior)
    grid_spec = pltpu.PrefetchScalarGridSpec(
        num_scalar_prefetch=1,
        grid=(count, qblocks),
        in_specs=in_specs,
        out_specs=pl.BlockSpec((1, BLK, lane_width), lambda s, b, idx: (s + first, b, 0)),
    )
    heads_here = lane_width // HEAD_DIM
    return pl.pallas_call(
        sparse_kernel,
        grid_spec=grid_spec,
        out_shape=jax.ShapeDtypeStruct(sparse_query.shape, sparse_query.dtype),
        input_output_aliases=aliases,
        compiler_params=pltpu.CompilerParams(dimension_semantics=("parallel", "parallel")),
        cost_estimate=pl.CostEstimate(
            flops=4 * count * qblocks * heads_here * BLK * SEL * BLK * HEAD_DIM,
            transcendentals=count * qblocks * heads_here * BLK * SEL * BLK,
            bytes_accessed=2 * 2 * count * tok_count * lane_width + 4 * count * qblocks * SEL * BLK * kv_width,
        ),
    )(store_index, *operands)


def body(
    lin_query, lin_key, lin_value, lin_gain, sparse_query, sparse_key, sparse_value, block_lists
):
    seq_count, tok_count, lane_width = lin_query.shape
    heads_here = lane_width // HEAD_DIM
    ctx_pos = lax.axis_index("z") * lax.axis_size("y") + lax.axis_index("y")
    queries = lin_query.reshape(seq_count, tok_count, heads_here, HEAD_DIM)
    key_rows = lin_key.reshape(seq_count, tok_count, heads_here, HEAD_DIM)
    value_rows = lin_value.reshape(seq_count, tok_count, heads_here, HEAD_DIM)
    states = jnp.einsum("sjhd,sjhe->shde", key_rows, value_rows, preferred_element_type=jnp.float32)
    kv_width = sparse_key.shape[2]
    qblocks = tok_count // BLK
    ctx_count = lax.axis_size("z") * lax.axis_size("y")
    store, store_index = listed_blocks(sparse_key, sparse_value, block_lists, ctx_pos, ctx_count)
    inside = linear_inside(lin_query, lin_key, lin_value)
    states, store, inside = lax.optimization_barrier((states, store, inside))
    offsets = jnp.arange(BLK, dtype=jnp.int32)
    query_pos = ((ctx_pos * qblocks + jnp.arange(qblocks, dtype=jnp.int32)) * BLK)[:, None] + offsets[None, :]
    key_pos = (block_lists[:, :, :, None] * BLK + offsets).reshape(seq_count, qblocks, 1, SEL * BLK)
    query_pos = query_pos[:, :, None]

    def first_part():
        return sparse_attend(sparse_query, store, store_index, key_pos, query_pos, 0, 1)

    def second_part(prior):
        return sparse_attend(sparse_query, store, store_index, key_pos, query_pos, 1, 1, prior)

    def third_part(prior):
        return sparse_attend(sparse_query, store, store_index, key_pos, query_pos, 2, seq_count - 2, prior)

    earlier, sparse_out = earlier_states(states, first_part, second_part, third_part)
    combined, row_squares = linear_finish(inside, lin_query, earlier)
    local_squares = row_squares[:, :, 0]
    whole_squares = local_squares
    head_count = lax.axis_size("head")
    step = 1
    while step < head_count:
        pairs = [(i, i ^ step) for i in range(head_count)]
        whole_squares = whole_squares + lax.ppermute(whole_squares, "head", pairs)
        step *= 2
    inv_rms = lax.rsqrt(whole_squares / (HEADS * HEAD_DIM) + norm_eps)
    lin_out = (combined * inv_rms[:, :, None] * lin_gain).astype(jnp.bfloat16)
    return (lin_out, sparse_out)


def solution(mesh):
    in_specs = (
        P(None, "ctx", "head"),
        P(None, "ctx", "head"),
        P(None, "ctx", "head"),
        P("head"),
        P(None, "ctx", "head"),
        P(None, "ctx", "head"),
        P(None, "ctx", "head"),
        P(None, "ctx", None),
    )
    out_specs = (P(None, "ctx", "head"), P(None, "ctx", "head"))
    n_ctx, n_head = mesh.devices.shape
    y_count = 4 if n_ctx % 4 == 0 else 1
    grid = Mesh(mesh.devices.reshape(n_ctx // y_count, y_count, n_head), ("z", "y", "head"))

    def split(spec):
        return P(*[("z", "y") if part == "ctx" else part for part in spec])

    return jax.shard_map(
        body,
        mesh=grid,
        in_specs=tuple(split(s) for s in in_specs),
        out_specs=tuple(split(s) for s in out_specs),
        check_vma=False,
    )
```

```python
import math

import jax
import jax.numpy as jnp
from jax import lax
from jax.experimental import pallas as pl
from jax.experimental.pallas import tpu as pltpu
from jax.sharding import Mesh, PartitionSpec as P

HEADS = 64
HEAD_DIM = 128
BLK = 64
SEL = 8
CAP = 2


norm_eps = 1e-05


def earlier_states(states, cover_first, cover_second, cover_third):
    y_pos = lax.axis_index("y")
    y_count = lax.axis_size("y")
    z_count = lax.axis_size("z")
    seq_count, heads_here, rows, cols = states.shape
    part_rows = rows // y_count
    quarters = states.reshape(seq_count, heads_here, y_count, part_rows, cols)

    def quarter(array, index):
        return lax.dynamic_index_in_dim(array, index, axis=2, keepdims=False)

    def cyclic(x, shift):
        return lax.ppermute(x, "y", [(i, (i + shift) % y_count) for i in range(y_count)])

    held = [quarter(quarters, y_pos)]
    for shift in range(1, y_count):
        held.append(cyclic(quarter(quarters, (y_pos + shift) % y_count), shift))
    held, cover_first = lax.optimization_barrier((held, cover_first()))
    sources = [(y_pos - shift) % y_count for shift in range(y_count)]
    group_total = sum(held[1:], held[0])
    below = []
    for shift in range(1, z_count):
        pairs = [(i, i + shift) for i in range(z_count - shift)]
        below.append(lax.ppermute(group_total, "z", pairs))
    below, covered = lax.optimization_barrier((below, cover_second(cover_first)))
    from_below = sum(below[1:], below[0])
    finished = []
    for target in range(y_count):
        within = from_below
        for source, piece in zip(sources, held):
            within = within + jnp.where(source < target, piece, 0.0)
        finished.append(within.astype(jnp.bfloat16))
    stacked = jnp.stack(finished)
    returned = [lax.dynamic_index_in_dim(stacked, y_pos, axis=0, keepdims=False)]
    for shift in range(1, y_count):
        outgoing = lax.dynamic_index_in_dim(stacked, (y_pos + shift) % y_count, axis=0, keepdims=False)
        returned.append(cyclic(outgoing, shift))
    returned, covered = lax.optimization_barrier((returned, cover_third(covered)))
    by_shift = jnp.stack(returned)
    order = (y_pos - jnp.arange(y_count)) % y_count
    by_quarter = jnp.take(by_shift, order, axis=0)
    return jnp.moveaxis(by_quarter, 0, 2).reshape(seq_count, heads_here, rows, cols), covered


def listed_blocks(sparse_key, sparse_value, block_lists, ctx_pos, ctx_count, tie):
    seq_count, tok_count, kv_width = sparse_key.shape
    qblocks = tok_count // BLK
    kv_blocks = jnp.stack(
        [sparse_key.reshape(seq_count, qblocks, BLK, kv_width),
         sparse_value.reshape(seq_count, qblocks, BLK, kv_width)],
        axis=2,
    )
    own_lists = block_lists.reshape(seq_count, qblocks * SEL)
    listed_here = jnp.any(
        own_lists[:, :, None] == jnp.arange(ctx_count * qblocks, dtype=jnp.int32), axis=1
    ).reshape(seq_count, ctx_count, qblocks)
    rank = jnp.cumsum(listed_here.astype(jnp.int32), axis=-1)
    wanted = jnp.stack(
        [jnp.argmax(listed_here & (rank == slot + 1), axis=-1) for slot in range(CAP)], axis=-1
    ).astype(jnp.int32)
    requests = jnp.moveaxis(wanted, 1, 0)
    asked = lax.all_to_all(requests, ("z", "y"), 0, 0, tiled=True)
    asked, tie = lax.optimization_barrier((asked, tie))
    send_index = (asked + jnp.arange(seq_count, dtype=jnp.int32)[None, :, None] * qblocks).reshape(-1)
    outgoing = jnp.take(kv_blocks.reshape(seq_count * qblocks, 2, BLK, kv_width), send_index, axis=0)
    arrived = lax.all_to_all(outgoing, ("z", "y"), 0, 0, tiled=True)
    store = jnp.concatenate(
        [kv_blocks.reshape(seq_count * qblocks, 2, BLK, kv_width), arrived], axis=0
    )
    own_rank = (rank - 1).reshape(seq_count, ctx_count * qblocks)
    slot = jnp.take_along_axis(own_rank, own_lists, axis=1)
    source = own_lists // qblocks
    local = own_lists % qblocks
    seq_ids = jnp.arange(seq_count, dtype=jnp.int32)[:, None]
    remote = seq_count * qblocks + (source * seq_count + seq_ids) * CAP + slot
    store_index = jnp.where(source == ctx_pos, seq_ids * qblocks + local, remote)
    store_index = jnp.clip(store_index, 0, store.shape[0] - 1)
    return store, store_index.astype(jnp.int32), tie


def _dot(a, b, contract):
    return lax.dot_general(a, b, (contract, ((), ())), preferred_element_type=jnp.float32)


def inside_kernel(q_ref, k_ref, v_ref, out_ref):
    scores = _dot(q_ref[0], k_ref[0], ((1,), (1,)))
    rows = lax.broadcasted_iota(jnp.int32, scores.shape, 0)
    cols = lax.broadcasted_iota(jnp.int32, scores.shape, 1)
    weights = jnp.where(rows >= cols, scores, 0.0).astype(jnp.bfloat16)
    out_ref[0] = _dot(weights, v_ref[0], ((1,), (0,)))


def finish_kernel(inside_ref, q_ref, e_ref, out_ref, sq_ref):
    heads_here = e_ref.shape[1]
    total = None
    for h in range(heads_here):
        lanes = slice(h * HEAD_DIM, (h + 1) * HEAD_DIM)
        combined = inside_ref[0, :, lanes] + _dot(q_ref[0, :, lanes], e_ref[0, h], ((1,), (0,)))
        out_ref[0, :, lanes] = combined
        squares = jnp.sum(combined * combined, axis=1, keepdims=True)
        total = squares if total is None else total + squares
    sq_ref[0] = total


def linear_inside(lin_query, lin_key, lin_value):
    seq_count, tok_count, lane_width = lin_query.shape
    heads_here = lane_width // HEAD_DIM
    tile = pl.BlockSpec((1, tok_count, HEAD_DIM), lambda s, h: (s, 0, h))
    return pl.pallas_call(
        inside_kernel,
        grid=(seq_count, heads_here),
        in_specs=[tile, tile, tile],
        out_specs=tile,
        out_shape=jax.ShapeDtypeStruct((seq_count, tok_count, lane_width), jnp.float32),
        compiler_params=pltpu.CompilerParams(dimension_semantics=("parallel", "parallel")),
        cost_estimate=pl.CostEstimate(
            flops=4 * seq_count * heads_here * tok_count * tok_count * HEAD_DIM,
            transcendentals=0,
            bytes_accessed=seq_count * tok_count * lane_width * (3 * 2 + 4),
        ),
    )(lin_query, lin_key, lin_value)


def linear_finish(inside, lin_query, earlier):
    seq_count, tok_count, lane_width = lin_query.shape
    heads_here = lane_width // HEAD_DIM
    rows = pl.BlockSpec((1, tok_count, lane_width), lambda s: (s, 0, 0))
    return pl.pallas_call(
        finish_kernel,
        grid=(seq_count,),
        in_specs=[rows, rows, pl.BlockSpec((1, heads_here, HEAD_DIM, HEAD_DIM), lambda s: (s, 0, 0, 0))],
        out_specs=[rows, pl.BlockSpec((1, tok_count, 1), lambda s: (s, 0, 0))],
        out_shape=[
            jax.ShapeDtypeStruct((seq_count, tok_count, lane_width), jnp.float32),
            jax.ShapeDtypeStruct((seq_count, tok_count, 1), jnp.float32),
        ],
        compiler_params=pltpu.CompilerParams(dimension_semantics=("parallel",)),
        cost_estimate=pl.CostEstimate(
            flops=2 * seq_count * heads_here * tok_count * HEAD_DIM * HEAD_DIM,
            transcendentals=0,
            bytes_accessed=seq_count * tok_count * lane_width * (2 + 4 + 4),
        ),
    )(inside, lin_query, earlier)


def sparse_kernel(index_ref, q_ref, *refs):
    block_refs = refs[:SEL]
    kpos_ref, qpos_ref, out_ref = refs[SEL], refs[SEL + 1], refs[-1]
    keys = jnp.concatenate([r[0, 0] for r in block_refs], axis=0)
    values = jnp.concatenate([r[0, 1] for r in block_refs], axis=0)
    heads_here = q_ref.shape[2] // HEAD_DIM
    queries = jnp.concatenate(
        [q_ref[0, :, h * HEAD_DIM:(h + 1) * HEAD_DIM] for h in range(heads_here)], axis=0
    )
    scores = _dot(queries, keys, ((1,), (1,))) * (1.0 / math.sqrt(HEAD_DIM))
    visible = kpos_ref[0, 0] <= qpos_ref[0]
    visible = jnp.concatenate([visible] * heads_here, axis=0)
    scores = jnp.where(visible, scores, -jnp.inf)
    row_max = jnp.max(scores, axis=1, keepdims=True)
    expo = jnp.exp(scores - row_max)
    probs = (expo / jnp.sum(expo, axis=1, keepdims=True)).astype(jnp.bfloat16)
    mixed = _dot(probs, values, ((1,), (0,))).astype(out_ref.dtype)
    rows = q_ref.shape[1]
    for h in range(heads_here):
        out_ref[0, :, h * HEAD_DIM:(h + 1) * HEAD_DIM] = mixed[h * rows:(h + 1) * rows]


def sparse_attend(sparse_query, store, store_index, key_pos, query_pos, first, count, prior=None):
    seq_count, tok_count, lane_width = sparse_query.shape
    qblocks = tok_count // BLK
    kv_width = store.shape[-1]

    def listed(j):
        return pl.BlockSpec(
            (1, 2, BLK, kv_width), lambda s, b, idx: (idx[s + first, b * SEL + j], 0, 0, 0)
        )

    in_specs = (
        [pl.BlockSpec((1, BLK, lane_width), lambda s, b, idx: (s + first, b, 0))]
        + [listed(j) for j in range(SEL)]
        + [
            pl.BlockSpec((1, 1, 1, SEL * BLK), lambda s, b, idx: (s + first, b, 0, 0)),
            pl.BlockSpec((1, BLK, 1), lambda s, b, idx: (b, 0, 0)),
        ]
    )
    operands = [sparse_query] + [store] * SEL + [key_pos, query_pos]
    aliases = {}
    if prior is not None:
        in_specs.append(pl.BlockSpec(memory_space=pl.ANY))
        aliases = {1 + len(operands): 0}
        operands.append(prior)
    grid_spec = pltpu.PrefetchScalarGridSpec(
        num_scalar_prefetch=1,
        grid=(count, qblocks),
        in_specs=in_specs,
        out_specs=pl.BlockSpec((1, BLK, lane_width), lambda s, b, idx: (s + first, b, 0)),
    )
    heads_here = lane_width // HEAD_DIM
    return pl.pallas_call(
        sparse_kernel,
        grid_spec=grid_spec,
        out_shape=jax.ShapeDtypeStruct(sparse_query.shape, sparse_query.dtype),
        input_output_aliases=aliases,
        compiler_params=pltpu.CompilerParams(dimension_semantics=("parallel", "parallel")),
        cost_estimate=pl.CostEstimate(
            flops=4 * count * qblocks * heads_here * BLK * SEL * BLK * HEAD_DIM,
            transcendentals=count * qblocks * heads_here * BLK * SEL * BLK,
            bytes_accessed=2 * 2 * count * tok_count * lane_width + 4 * count * qblocks * SEL * BLK * kv_width,
        ),
    )(store_index, *operands)


def body(
    lin_query, lin_key, lin_value, lin_gain, sparse_query, sparse_key, sparse_value, block_lists
):
    seq_count, tok_count, lane_width = lin_query.shape
    heads_here = lane_width // HEAD_DIM
    ctx_pos = lax.axis_index("z") * lax.axis_size("y") + lax.axis_index("y")
    queries = lin_query.reshape(seq_count, tok_count, heads_here, HEAD_DIM)
    key_rows = lin_key.reshape(seq_count, tok_count, heads_here, HEAD_DIM)
    value_rows = lin_value.reshape(seq_count, tok_count, heads_here, HEAD_DIM)
    states = jnp.einsum("sjhd,sjhe->shde", key_rows, value_rows, preferred_element_type=jnp.float32)
    kv_width = sparse_key.shape[2]
    qblocks = tok_count // BLK
    ctx_count = lax.axis_size("z") * lax.axis_size("y")
    store, store_index, states = listed_blocks(sparse_key, sparse_value, block_lists, ctx_pos, ctx_count, states)
    inside = linear_inside(lin_query, lin_key, lin_value)
    states, store, inside = lax.optimization_barrier((states, store, inside))
    offsets = jnp.arange(BLK, dtype=jnp.int32)
    query_pos = ((ctx_pos * qblocks + jnp.arange(qblocks, dtype=jnp.int32)) * BLK)[:, None] + offsets[None, :]
    key_pos = (block_lists[:, :, :, None] * BLK + offsets).reshape(seq_count, qblocks, 1, SEL * BLK)
    query_pos = query_pos[:, :, None]

    def first_part():
        return sparse_attend(sparse_query, store, store_index, key_pos, query_pos, 0, 1)

    def second_part(prior):
        return sparse_attend(sparse_query, store, store_index, key_pos, query_pos, 1, 1, prior)

    def third_part(prior):
        return sparse_attend(sparse_query, store, store_index, key_pos, query_pos, 2, seq_count - 2, prior)

    earlier, sparse_out = earlier_states(states, first_part, second_part, third_part)
    combined, row_squares = linear_finish(inside, lin_query, earlier)
    local_squares = row_squares[:, :, 0]
    whole_squares = local_squares
    head_count = lax.axis_size("head")
    step = 1
    while step < head_count:
        pairs = [(i, i ^ step) for i in range(head_count)]
        whole_squares = whole_squares + lax.ppermute(whole_squares, "head", pairs)
        step *= 2
    inv_rms = lax.rsqrt(whole_squares / (HEADS * HEAD_DIM) + norm_eps)
    lin_out = (combined * inv_rms[:, :, None] * lin_gain).astype(jnp.bfloat16)
    return (lin_out, sparse_out)


def solution(mesh):
    in_specs = (
        P(None, "ctx", "head"),
        P(None, "ctx", "head"),
        P(None, "ctx", "head"),
        P("head"),
        P(None, "ctx", "head"),
        P(None, "ctx", "head"),
        P(None, "ctx", "head"),
        P(None, "ctx", None),
    )
    out_specs = (P(None, "ctx", "head"), P(None, "ctx", "head"))
    n_ctx, n_head = mesh.devices.shape
    y_count = 4 if n_ctx % 4 == 0 else 1
    grid = Mesh(mesh.devices.reshape(n_ctx // y_count, y_count, n_head), ("z", "y", "head"))

    def split(spec):
        return P(*[("z", "y") if part == "ctx" else part for part in spec])

    return jax.shard_map(
        body,
        mesh=grid,
        in_specs=tuple(split(s) for s in in_specs),
        out_specs=tuple(split(s) for s in out_specs),
        check_vma=False,
    )
```
